32 devices in a mesh: seq: 16 (over z, y, core), dp: 2 (over x).
Axes of the slice: x: 2, y: 2, z: 4, core: 2. Of those that a mesh axis runs over, the one named last changes fastest.
Arguments:
- query_rows: bfloat16 [2, 4096, 768], P('dp', 'seq'), may hold values from -40 to 40
- key_rows: bfloat16 [2, 4096, 768], P('dp', 'seq'), may hold values from -40 to 40
- value_rows: bfloat16 [2, 4096, 768], P('dp', 'seq'), may hold values from -6 to 6
- out_grad: bfloat16 [2, 4096, 1536], P('dp', 'seq'), may hold values from -6 to 6
- lengths: int32 [2, 8], P('dp'), may hold values from 1 to 1024, 4096 in all within a row
- out_weight: bfloat16 [768, 1536], P('seq', 'dp'), may hold values from -0.21875 to 0.21875
Outputs:
- mixed_out: bfloat16 [2, 4096, 1536], P('dp', 'seq')
- query_grad: bfloat16 [2, 4096, 768], P('dp', 'seq')
- key_grad: bfloat16 [2, 4096, 768], P('dp', 'seq')
- value_grad: bfloat16 [2, 4096, 768], P('dp', 'seq')
- weight_grad: float32 [768, 1536], P('seq', 'dp')
The draws below stay inside these ranges and needn't reach their ends.
Inputs may be any that keep to these rules, and one draw needn't show every extreme that they name: Each row holds the lengths of the 8 utterances of one group in packing order; they sum to 4096 and the longest is exactly 1024.
All inputs are finite; a program needn't handle non-finite values.
Results may differ from the reference program's by a relative error of at most 0.022.
Values may be sent and summed in bfloat16 or wider, within the bound.
No kernel may reach another device: no remote copies, remote signals or barrier semaphores. Data moves between devices by JAX's collectives and lax.ppermute only.
A program may use at most 64 MiB of HBM per device.

```python
import math
import jax
import jax.numpy as jnp
import numpy as np
from jax import lax

D = 1536
HEADS = 12
HEAD_DIM = 64
STRETCH = 128
MOST = 1024
HD = 768
FRAMES = 4096
GROUPS = 2
UTTS = 8


def draw_query_rows(key, part):
    drawn = jnp.clip(jax.random.normal(jax.random.fold_in(key, 21), (GROUPS, FRAMES, HD), jnp.float32), -6.0, 6.0)
    return drawn.astype(jnp.bfloat16)


def draw_key_rows(key, part):
    drawn = jnp.clip(jax.random.normal(jax.random.fold_in(key, 22), (GROUPS, FRAMES, HD), jnp.float32), -6.0, 6.0)
    return drawn.astype(jnp.bfloat16)


def with_spikes(result, rng, source, target, shards_of, factor):
    owner, partner = [(jnp.arange(result.shape[axis_at]) // (result.shape[axis_at] // shards_of)).reshape([-1 if axis == axis_at else 1 for axis in range(result.ndim)]) for axis_at in (source, target)]
    chosen = jax.random.permutation(rng, shards_of)[partner]
    strong = (owner == chosen) | (owner == (partner + shards_of // 2) % shards_of)
    return jnp.where(strong, factor * result, result)


def shard_levels(stream_key, shape, split, low, high):
    def one(axis_at, shards_of):
        draws = jax.random.uniform(jax.random.fold_in(jax.random.fold_in(stream_key, 6), axis_at), (shards_of,), jnp.float32, low / len(split), high / len(split))
        return jnp.repeat(jnp.exp(draws), shape[axis_at] // shards_of).reshape((-1,) + (1,) * (len(shape) - axis_at - 1))

    factor_of = one(*split[0])
    for cut in split[1:]:
        factor_of = factor_of * one(*cut)
    return factor_of


def split_up(amount, total, most, lean):
    loads = [(1 << 20) // math.isqrt(rank ** lean) + 1 for rank in range(2, amount + 1)]
    spare, holding = total - most - (amount - 1), [1] * (amount - 1)
    while spare > 0:
        free = [i for i in range(amount - 1) if holding[i] < most]
        mass, remaining = sum([loads[i] for i in free]), spare
        for i in free:
            addition = min(most - holding[i], max(1, remaining * loads[i] // mass), spare)
            holding[i] = holding[i] + addition
            spare = spare - addition
    return np.array([most] + holding)


def ragged_sizes(stream_key, amount, total, most, lean):
    if amount == 2:
        one = jax.random.randint(stream_key, (), max(1, total - most), min(most, total - 1) + 1)
        return jnp.stack([one, total - one])
    sizes = jnp.asarray(split_up(amount, total, most, lean), jnp.int32)
    couples = (amount - 1) // 2
    giver, taker = sizes[1:1 + 2 * couples:2], sizes[2:2 + 2 * couples:2]
    margin = jnp.minimum(giver - 1, most - taker)
    passed = jax.random.randint(jax.random.fold_in(stream_key, 1), (couples,), 0, 1 << 20) % (margin + 1)
    sizes = sizes.at[1:1 + 2 * couples:2].set(giver - passed).at[2:2 + 2 * couples:2].set(taker + passed)
    return sizes[jax.random.permutation(jax.random.fold_in(stream_key, 2), amount)]


def gaussian(stream_key, shape, scale, most, cuts=(), kind=jnp.bfloat16):
    drawn = scale * jax.random.normal(stream_key, shape, jnp.float32)
    if cuts:
        drawn = drawn * shard_levels(stream_key, shape, cuts, -0.22, 0.18)
    return jnp.clip(drawn, -most, most).astype(kind)


def noise_with(key, shape, scale, limit, cuts, heavy, kind=jnp.bfloat16):
    result = scale * jax.random.normal(key, shape, jnp.float32)
    if cuts:
        result = result * shard_levels(key, shape, cuts, -0.22, 0.18)
    return jnp.clip(with_spikes(result, jax.random.fold_in(key, 3), *heavy), -limit, limit).astype(kind)


def setup_inputs(seed: int = 0) -> dict:
    seeds = jax.random.split(jax.random.key(seed), 7)
    return {
        "query_rows": draw_query_rows(jax.random.fold_in(seeds[6], 71), 0),
        "key_rows": draw_key_rows(jax.random.fold_in(seeds[6], 71), 0),
        "value_rows": noise_with(seeds[2], (GROUPS, FRAMES, HD), 1.0, 6.0, ((0, 2), (1, 16)), (1, 2, 16, 2.0)),
        "out_grad": noise_with(seeds[3], (GROUPS, FRAMES, D), 1.0, 6.0, ((0, 2), (1, 16)), (0, 2, 2, 2.0)),
        "lengths": jax.vmap(lambda own: ragged_sizes(own, UTTS, FRAMES, MOST, 2))(jax.random.split(seeds[4], GROUPS)).reshape((GROUPS, UTTS)).astype(jnp.int32),
        "out_weight": gaussian(seeds[5], (HD, D), HD ** -0.5, 0.21875, ((0, 16), (1, 2))),
    }


MASKED_SCORE = -1e30


def rounded(values_in):
    return lax.optimization_barrier(values_in.astype(jnp.bfloat16)).astype(jnp.float32)


def utterance_of(utt_lengths, positions):
    utt_ends = jnp.cumsum(utt_lengths)
    utt_index = jnp.sum((positions[:, None] >= utt_ends[None, :]).astype(jnp.int32), axis=1)
    return jnp.where(positions < 0, -1, utt_index).astype(jnp.int32)


def group_pass(query_in, key_in, value_in, upstream, utt_lengths, out_weight):
    frame_count = query_in.shape[0]
    block_rows = min(512, frame_count)
    block_count = frame_count // block_rows
    window_rows = MOST + block_rows
    score_scale = HEAD_DIM ** -0.5
    positions = jnp.arange(frame_count, dtype=jnp.int32)
    query_utt = utterance_of(utt_lengths, positions)
    query_stretch = positions // STRETCH
    key_pos = jnp.arange(MOST + frame_count, dtype=jnp.int32) - MOST
    key_utt = utterance_of(utt_lengths, key_pos)
    key_stretch = key_pos // STRETCH
    query_heads = query_in.reshape(frame_count, HEADS, HEAD_DIM).astype(jnp.float32)
    padding = jnp.zeros((MOST, HEADS, HEAD_DIM), jnp.float32)
    key_heads = jnp.concatenate([padding, key_in.reshape(frame_count, HEADS, HEAD_DIM).astype(jnp.float32)], 0)
    value_heads = jnp.concatenate([padding, value_in.reshape(frame_count, HEADS, HEAD_DIM).astype(jnp.float32)], 0)

    def pieces(block_index):
        offset = (block_index * block_rows).astype(jnp.int32)
        query_block = lax.dynamic_slice_in_dim(query_heads, offset, block_rows, 0)
        key_block = lax.dynamic_slice_in_dim(key_heads, offset, window_rows, 0)
        value_block = lax.dynamic_slice_in_dim(value_heads, offset, window_rows, 0)
        utt_query = lax.dynamic_slice_in_dim(query_utt, offset, block_rows, 0)
        stretch_query = lax.dynamic_slice_in_dim(query_stretch, offset, block_rows, 0)
        utt_key = lax.dynamic_slice_in_dim(key_utt, offset, window_rows, 0)
        stretch_key = lax.dynamic_slice_in_dim(key_stretch, offset, window_rows, 0)
        visible = (utt_query[:, None] == utt_key[None, :]) & (stretch_key[None, :] <= stretch_query[:, None])
        scores = jnp.einsum('qhe,khe->hqk', query_block, key_block) * score_scale
        return offset, query_block, key_block, value_block, visible, scores

    def forward_block(block_index):
        offset, query_block, key_block, value_block, visible, scores = pieces(block_index)
        scores = jnp.where(visible[None], scores, MASKED_SCORE)
        top_score = jnp.max(scores, axis=2)
        expo_full = jnp.where(visible[None], jnp.exp(scores - top_score[:, :, None]), 0.0)
        row_sum = jnp.sum(expo_full, axis=2)
        prob_bf = rounded(expo_full)
        weighted = jnp.einsum('hqk,khe->qhe', prob_bf, value_block) / jnp.transpose(row_sum)[:, :, None]
        return weighted.reshape(block_rows, HEADS * HEAD_DIM).astype(jnp.bfloat16), top_score + jnp.log(row_sum)

    block_ids = jnp.arange(block_count, dtype=jnp.int32)
    out_blocks, log_sums = lax.map(forward_block, block_ids)
    attended = out_blocks.reshape(frame_count, HEADS * HEAD_DIM)
    mixed_out = jnp.dot(attended, out_weight, preferred_element_type=jnp.float32).astype(jnp.bfloat16)
    att_grad = jnp.dot(upstream, out_weight.T, preferred_element_type=jnp.float32).astype(jnp.bfloat16)
    att_grad_heads = att_grad.reshape(frame_count, HEADS, HEAD_DIM).astype(jnp.float32)
    delta_rows = jnp.sum(att_grad_heads * attended.reshape(frame_count, HEADS, HEAD_DIM).astype(jnp.float32), axis=2)

    def backward_block(carried, block_index):
        key_acc, value_acc = carried
        offset, query_block, key_block, value_block, visible, scores = pieces(block_index)
        log_sum = log_sums[block_index]
        grad_block = lax.dynamic_slice_in_dim(att_grad_heads, offset, block_rows, 0)
        delta_block = lax.dynamic_slice_in_dim(delta_rows, offset, block_rows, 0)
        prob_full = jnp.where(visible[None], jnp.exp(scores - log_sum[:, :, None]), 0.0)
        prob_back = rounded(prob_full)
        prob_grad = jnp.einsum('qhe,khe->hqk', grad_block, value_block)
        score_grad = rounded(prob_full * (prob_grad - jnp.transpose(delta_block)[:, :, None]))
        query_part = jnp.einsum('hqk,khe->qhe', score_grad, key_block) * score_scale
        key_part = jnp.einsum('hqk,qhe->khe', score_grad, query_block) * score_scale
        value_part = jnp.einsum('hqk,qhe->khe', prob_back, grad_block)
        key_acc = lax.dynamic_update_slice_in_dim(key_acc, lax.dynamic_slice_in_dim(key_acc, offset, window_rows, 0) + key_part, offset, 0)
        value_acc = lax.dynamic_update_slice_in_dim(value_acc, lax.dynamic_slice_in_dim(value_acc, offset, window_rows, 0) + value_part, offset, 0)
        return (key_acc, value_acc), query_part.reshape(block_rows, HEADS * HEAD_DIM).astype(jnp.bfloat16)

    zero_grads = jnp.zeros((MOST + frame_count, HEADS, HEAD_DIM), jnp.float32)
    (key_acc, value_acc), query_parts = lax.scan(backward_block, (zero_grads, zero_grads), block_ids)
    query_grad = query_parts.reshape(frame_count, HEADS * HEAD_DIM)
    key_grad = key_acc[MOST:].reshape(frame_count, HEADS * HEAD_DIM).astype(jnp.bfloat16)
    value_grad = value_acc[MOST:].reshape(frame_count, HEADS * HEAD_DIM).astype(jnp.bfloat16)
    weight_term = jnp.dot(attended.T, upstream, preferred_element_type=jnp.float32)
    return mixed_out, query_grad, key_grad, value_grad, weight_term


def reference(query_rows, key_rows, value_rows, out_grad, lengths, out_weight):
    def per_group(group_items):
        query_in, key_in, value_in, upstream, utt_lengths = group_items
        return group_pass(query_in, key_in, value_in, upstream, utt_lengths, out_weight)

    mixed_out, query_grad, key_grad, value_grad, group_terms = lax.map(per_group, (query_rows, key_rows, value_rows, out_grad, lengths))
    return mixed_out, query_grad, key_grad, value_grad, jnp.sum(group_terms, axis=0)
```

```python
import jax
import jax.numpy as jnp
from jax import lax
from jax.sharding import PartitionSpec as P

HEADS = 12
HEAD_DIM = 64
STRETCH = 128
MOST = 1024


MASKED_SCORE = -1e30


def shift_up(block, axis, distance):
    devices = range(lax.axis_size(axis))
    route = [(i - distance, i) for i in devices if i - distance in devices]
    return lax.ppermute(block, axis, route)


def frame_labels(utt_lengths, first_frame, frame_count, total_frames):
    positions = first_frame + jnp.arange(frame_count, dtype=jnp.int32)
    utt_ends = jnp.cumsum(utt_lengths)
    utt_index = jnp.sum((positions[:, None] >= utt_ends[None, :]).astype(jnp.int32), axis=1)
    outside = (positions < 0) | (positions >= total_frames)
    return (jnp.where(outside, -1, utt_index), positions // STRETCH)


def local(query_rows, key_rows, value_rows, out_grad, lengths, out_weight):
    seq_count = lax.axis_size("seq")
    device = lax.axis_index("seq")
    tok_rows = query_rows.shape[1]
    feature_width = query_rows.shape[2]
    total_frames = seq_count * tok_rows
    reach = min(-(-MOST // tok_rows), seq_count - 1)
    window = (reach + 1) * tok_rows
    score_scale = HEAD_DIM ** (-0.5)
    utt_lengths = lengths[0]

    weight_cols = lax.all_gather(out_weight, "dp", axis=1, tiled=True)
    weight_full = lax.all_gather(weight_cols, "seq", axis=0, tiled=True)

    query_heads = query_rows[0].reshape(tok_rows, HEADS, HEAD_DIM)
    key_value = jnp.concatenate([key_rows[0], value_rows[0]], axis=1)

    held = [key_value]
    for _ in range(reach):
        held.append(shift_up(held[-1], "seq", 1))
    kv_window = jnp.concatenate(held[::-1], axis=0)
    key_window = kv_window[:, :feature_width].reshape(window, HEADS, HEAD_DIM)
    value_window = kv_window[:, feature_width:].reshape(window, HEADS, HEAD_DIM)

    query_utt, query_stretch = frame_labels(utt_lengths, device * tok_rows, tok_rows, total_frames)
    key_utt, key_stretch = frame_labels(
        utt_lengths, (device - reach) * tok_rows, window, total_frames
    )
    visible = (query_utt[:, None] == key_utt[None, :]) & (
        key_stretch[None, :] <= query_stretch[:, None]
    )

    scores = (
        jnp.einsum("qhe,khe->hqk", query_heads, key_window, preferred_element_type=jnp.float32)
        * score_scale
    )
    masked = jnp.where(visible[None], scores, MASKED_SCORE)
    top_score = jnp.max(masked, axis=2)
    expo_full = jnp.where(visible[None], jnp.exp(masked - top_score[:, :, None]), 0.0)
    row_sum = jnp.sum(expo_full, axis=2)
    weighted = jnp.einsum(
        "hqk,khe->qhe",
        expo_full.astype(jnp.bfloat16),
        value_window,
        preferred_element_type=jnp.float32,
    )
    attended = (
        (weighted / jnp.transpose(row_sum)[:, :, None])
        .reshape(tok_rows, feature_width)
        .astype(jnp.bfloat16)
    )
    log_sum = top_score + jnp.log(row_sum)

    mixed_out = jnp.dot(attended, weight_full, preferred_element_type=jnp.float32).astype(
        jnp.bfloat16
    )
    upstream = out_grad[0]
    att_grad = lax.dot_general(
        upstream, weight_full, (((1,), (1,)), ((), ())), preferred_element_type=jnp.float32
    ).astype(jnp.bfloat16)

    partial_weight = lax.dot_general(
        attended, upstream, (((0,), (0,)), ((), ())), preferred_element_type=jnp.float32
    )
    col_share = lax.psum_scatter(partial_weight, "dp", scatter_dimension=1, tiled=True)
    weight_grad = lax.psum_scatter(col_share, "seq", scatter_dimension=0, tiled=True)

    grad_heads = att_grad.reshape(tok_rows, HEADS, HEAD_DIM)
    delta_rows = jnp.sum(
        grad_heads.astype(jnp.float32)
        * attended.reshape(tok_rows, HEADS, HEAD_DIM).astype(jnp.float32),
        axis=2,
    )

    query_acc = jnp.zeros((tok_rows, HEADS, HEAD_DIM), jnp.float32)
    carried = None
    for back in range(reach, -1, -1):
        rows = slice((reach - back) * tok_rows, (reach - back + 1) * tok_rows)
        key_block = key_window[rows]
        value_block = value_window[rows]
        block_visible = visible[:, rows]
        block_scores = (
            jnp.einsum("qhe,khe->hqk", query_heads, key_block, preferred_element_type=jnp.float32)
            * score_scale
        )
        prob_full = jnp.where(
            block_visible[None], jnp.exp(block_scores - log_sum[:, :, None]), 0.0
        )
        prob_back = prob_full.astype(jnp.bfloat16)
        prob_grad = jnp.einsum(
            "qhe,khe->hqk", grad_heads, value_block, preferred_element_type=jnp.float32
        )
        score_grad = (prob_full * (prob_grad - jnp.transpose(delta_rows)[:, :, None])).astype(
            jnp.bfloat16
        )
        query_acc = query_acc + jnp.einsum(
            "hqk,khe->qhe", score_grad, key_block, preferred_element_type=jnp.float32
        )
        key_part = (
            jnp.einsum("hqk,qhe->khe", score_grad, query_heads, preferred_element_type=jnp.float32)
            * score_scale
        )
        value_part = jnp.einsum(
            "hqk,qhe->khe", prob_back, grad_heads, preferred_element_type=jnp.float32
        )
        part = jnp.concatenate(
            [key_part.reshape(tok_rows, feature_width), value_part.reshape(tok_rows, feature_width)],
            axis=1,
        )
        if carried is None:
            carried = part
        else:
            carried = shift_up(carried, "seq", -1) + part

    query_grad = (query_acc * score_scale).reshape(tok_rows, feature_width).astype(jnp.bfloat16)
    key_grad = carried[:, :feature_width].astype(jnp.bfloat16)
    value_grad = carried[:, feature_width:].astype(jnp.bfloat16)
    return (mixed_out[None], query_grad[None], key_grad[None], value_grad[None], weight_grad)


def solution(mesh):
    return jax.shard_map(
        local,
        mesh=mesh,
        in_specs=(
            P("dp", "seq", None),
            P("dp", "seq", None),
            P("dp", "seq", None),
            P("dp", "seq", None),
            P("dp", None),
            P("seq", "dp"),
        ),
        out_specs=(
            P("dp", "seq", None),
            P("dp", "seq", None),
            P("dp", "seq", None),
            P("dp", "seq", None),
            P("seq", "dp"),
        ),
        check_vma=False,
    )
```

```python
import jax
import jax.numpy as jnp
from jax import lax
from jax.sharding import PartitionSpec as P

HEADS = 12
HEAD_DIM = 64
STRETCH = 128
MOST = 1024


MASKED_SCORE = -1e30


def shift_up(block, axis, distance):
    devices = range(lax.axis_size(axis))
    route = [(i - distance, i) for i in devices if i - distance in devices]
    return lax.ppermute(block, axis, route)


def swap_partner(block, axis):
    count = lax.axis_size(axis)
    return lax.ppermute(block, axis, [(i, i ^ 1) for i in range(count)])


def frame_labels(utt_lengths, first_frame, frame_count, total_frames):
    positions = first_frame + jnp.arange(frame_count, dtype=jnp.int32)
    utt_ends = jnp.cumsum(utt_lengths)
    utt_index = jnp.sum((positions[:, None] >= utt_ends[None, :]).astype(jnp.int32), axis=1)
    outside = (positions < 0) | (positions >= total_frames)
    return (jnp.where(outside, -1, utt_index), positions // STRETCH)


def head_major(rows, tok_rows):
    return jnp.transpose(rows.reshape(tok_rows, HEADS, HEAD_DIM), (1, 0, 2))


def row_major(heads, tok_rows):
    return jnp.transpose(heads, (1, 0, 2)).reshape(tok_rows, HEADS * HEAD_DIM)


def gather_behind(own, reach, paired, core):
    if not paired:
        held = [own]
        for _ in range(reach):
            held.append(shift_up(held[-1], "seq", 1))
        return held
    evens = {0: own}
    for dist in range(2, reach + 2, 2):
        evens[dist] = shift_up(own, "seq", dist)
    odds = list(range(1, reach + 1, 2))
    payload = [jnp.where(core == 0, evens[s - 1], evens[s + 1]) for s in odds]
    received = swap_partner(payload, "seq")
    held = []
    for dist in range(reach + 1):
        held.append(evens[dist] if dist % 2 == 0 else received[(dist - 1) // 2])
    return held


def return_behind(parts, reach, paired, core):
    if not paired:
        carried = parts[reach]
        for dist in range(reach - 1, -1, -1):
            carried = shift_up(carried.astype(jnp.bfloat16), "seq", -1).astype(jnp.float32) + parts[dist]
        return carried
    odds = list(range(1, reach + 1, 2))
    received = swap_partner([parts[s] for s in odds], "seq")
    total = None
    for dist in range(0, reach + 2, 2):
        zero = jnp.zeros_like(parts[0])
        from_core1 = received[dist // 2] if dist // 2 < len(odds) else zero
        from_core0 = received[dist // 2 - 1] if dist >= 2 and dist // 2 - 1 < len(odds) else zero
        own = parts[dist] if dist <= reach else zero
        summed = own + jnp.where(core == 0, from_core1, from_core0)
        if dist == 0:
            total = summed
        else:
            total = total + shift_up(summed.astype(jnp.bfloat16), "seq", -dist).astype(jnp.float32)
    return total


def local(query_rows, key_rows, value_rows, out_grad, lengths, out_weight):
    seq_count = lax.axis_size("seq")
    device = lax.axis_index("seq")
    core = device % 2
    paired = seq_count % 2 == 0
    tok_rows = query_rows.shape[1]
    feature_width = query_rows.shape[2]
    total_frames = seq_count * tok_rows
    reach = min(-(-MOST // tok_rows), seq_count - 1)
    score_scale = HEAD_DIM ** (-0.5)
    utt_lengths = lengths[0]

    weight_cols = lax.all_gather(out_weight, "dp", axis=1, tiled=True)
    weight_full = lax.all_gather(weight_cols, "seq", axis=0, tiled=True)

    query_heads = head_major(query_rows[0], tok_rows)
    own_kv = jnp.stack([head_major(key_rows[0], tok_rows), head_major(value_rows[0], tok_rows)])
    held = gather_behind(own_kv, reach, paired, core)

    query_utt, query_stretch = frame_labels(utt_lengths, device * tok_rows, tok_rows, total_frames)
    block_visible = []
    for dist in range(reach + 1):
        key_utt, key_stretch = frame_labels(
            utt_lengths, (device - dist) * tok_rows, tok_rows, total_frames
        )
        block_visible.append(
            (query_utt[:, None] == key_utt[None, :]) & (key_stretch[None, :] <= query_stretch[:, None])
        )

    block_scores = []
    top_score = None
    for dist in range(reach + 1):
        scores = (
            jnp.einsum("hqe,hke->hqk", query_heads, held[dist][0], preferred_element_type=jnp.float32)
            * score_scale
        )
        scores = jnp.where(block_visible[dist][None], scores, MASKED_SCORE)
        block_scores.append(scores)
        block_top = jnp.max(scores, axis=2)
        top_score = block_top if top_score is None else jnp.maximum(top_score, block_top)
    row_sum = None
    weighted = None
    for dist in range(reach + 1):
        expo_full = jnp.where(
            block_visible[dist][None], jnp.exp(block_scores[dist] - top_score[:, :, None]), 0.0
        )
        part_sum = jnp.sum(expo_full, axis=2)
        product = jnp.einsum(
            "hqk,hke->hqe",
            expo_full.astype(jnp.bfloat16),
            held[dist][1],
            preferred_element_type=jnp.float32,
        )
        row_sum = part_sum if row_sum is None else row_sum + part_sum
        weighted = product if weighted is None else weighted + product
    attended_heads = (weighted / row_sum[:, :, None]).astype(jnp.bfloat16)
    attended = row_major(attended_heads, tok_rows)
    log_sum = top_score + jnp.log(row_sum)

    mixed_out = jnp.dot(attended, weight_full, preferred_element_type=jnp.float32).astype(
        jnp.bfloat16
    )
    upstream = out_grad[0]
    att_grad = lax.dot_general(
        upstream, weight_full, (((1,), (1,)), ((), ())), preferred_element_type=jnp.float32
    ).astype(jnp.bfloat16)

    partial_weight = lax.dot_general(
        attended, upstream, (((0,), (0,)), ((), ())), preferred_element_type=jnp.float32
    )
    row_share = lax.psum_scatter(
        partial_weight.astype(jnp.bfloat16), "seq", scatter_dimension=0, tiled=True
    )
    weight_grad = lax.psum_scatter(
        row_share.astype(jnp.float32), "dp", scatter_dimension=1, tiled=True
    )

    grad_heads = head_major(att_grad, tok_rows)
    delta_rows = jnp.sum(
        grad_heads.astype(jnp.float32) * attended_heads.astype(jnp.float32), axis=2
    )

    query_acc = None
    parts = [None] * (reach + 1)
    order = [d for d in range(reach, -1, -1) if d % 2 == 1] + [
        d for d in range(reach, -1, -1) if d % 2 == 0
    ]
    for dist in order:
        key_block = held[dist][0]
        value_block = held[dist][1]
        scores = (
            jnp.einsum("hqe,hke->hqk", query_heads, key_block, preferred_element_type=jnp.float32)
            * score_scale
        )
        prob_full = jnp.where(
            block_visible[dist][None], jnp.exp(scores - log_sum[:, :, None]), 0.0
        )
        prob_back = prob_full.astype(jnp.bfloat16)
        prob_grad = jnp.einsum(
            "hqe,hke->hqk", grad_heads, value_block, preferred_element_type=jnp.float32
        )
        score_grad = (prob_full * (prob_grad - delta_rows[:, :, None])).astype(jnp.bfloat16)
        query_part = jnp.einsum(
            "hqk,hke->hqe", score_grad, key_block, preferred_element_type=jnp.float32
        )
        query_acc = query_part if query_acc is None else query_acc + query_part
        key_part = (
            jnp.einsum("hqk,hqe->hke", score_grad, query_heads, preferred_element_type=jnp.float32)
            * score_scale
        )
        value_part = jnp.einsum(
            "hqk,hqe->hke", prob_back, grad_heads, preferred_element_type=jnp.float32
        )
        parts[dist] = jnp.stack([key_part, value_part])

    kv_grad = return_behind(parts, reach, paired, core)
    query_grad = row_major(query_acc * score_scale, tok_rows).astype(jnp.bfloat16)
    key_grad = row_major(kv_grad[0], tok_rows).astype(jnp.bfloat16)
    value_grad = row_major(kv_grad[1], tok_rows).astype(jnp.bfloat16)
    return (mixed_out[None], query_grad[None], key_grad[None], value_grad[None], weight_grad)


def solution(mesh):
    return jax.shard_map(
        local,
        mesh=mesh,
        in_specs=(
            P("dp", "seq", None),
            P("dp", "seq", None),
            P("dp", "seq", None),
            P("dp", "seq", None),
            P("dp", None),
            P("seq", "dp"),
        ),
        out_specs=(
            P("dp", "seq", None),
            P("dp", "seq", None),
            P("dp", "seq", None),
            P("dp", "seq", None),
            P("seq", "dp"),
        ),
        check_vma=False,
    )
```

```python
import jax
import jax.numpy as jnp
from jax import lax
from jax.sharding import PartitionSpec as P

HEADS = 12
HEAD_DIM = 64
STRETCH = 128
MOST = 1024


MASKED_SCORE = -1e30


def shift_up(block, axis, distance):
    devices = range(lax.axis_size(axis))
    route = [(i - distance, i) for i in devices if i - distance in devices]
    return lax.ppermute(block, axis, route)


def swap_partner(block, axis):
    count = lax.axis_size(axis)
    return lax.ppermute(block, axis, [(i, i ^ 1) for i in range(count)])


def halving_scatter(total, axis, dim, sends_narrow):
    count = lax.axis_size(axis)
    if count & (count - 1):
        return lax.psum_scatter(total, axis, scatter_dimension=dim, tiled=True)
    me = lax.axis_index(axis)
    bits = count.bit_length() - 1
    moved = jnp.moveaxis(total, dim, 0)
    rest = moved.shape[1:]
    blocks = moved.reshape((2,) * bits + (moved.shape[0] // count,) + rest)
    for step in range(bits):
        own_bit = (me >> step) % 2
        keep = lax.dynamic_index_in_dim(blocks, own_bit, blocks.ndim - len(rest) - 2, keepdims=False)
        give = lax.dynamic_index_in_dim(blocks, 1 - own_bit, blocks.ndim - len(rest) - 2, keepdims=False)
        if sends_narrow[step]:
            give = give.astype(jnp.bfloat16)
        got = lax.ppermute(give, axis, [(i, i ^ (1 << step)) for i in range(count)])
        blocks = keep + got.astype(keep.dtype)
    return jnp.moveaxis(blocks, 0, dim)


def frame_labels(utt_lengths, first_frame, frame_count, total_frames):
    positions = first_frame + jnp.arange(frame_count, dtype=jnp.int32)
    utt_ends = jnp.cumsum(utt_lengths)
    utt_index = jnp.sum((positions[:, None] >= utt_ends[None, :]).astype(jnp.int32), axis=1)
    outside = (positions < 0) | (positions >= total_frames)
    return (jnp.where(outside, -1, utt_index), positions // STRETCH)


def head_major(rows, tok_rows):
    return jnp.transpose(rows.reshape(tok_rows, HEADS, HEAD_DIM), (1, 0, 2))


def row_major(heads, tok_rows):
    return jnp.transpose(heads, (1, 0, 2)).reshape(tok_rows, HEADS * HEAD_DIM)


def gather_behind(own, reach, paired, core):
    if not paired:
        held = [own]
        for _ in range(reach):
            held.append(shift_up(held[-1], "seq", 1))
        return held
    evens = {0: own}
    for dist in range(2, reach + 2, 2):
        evens[dist] = shift_up(own, "seq", dist)
    odds = list(range(1, reach + 1, 2))
    payload = [jnp.where(core == 0, evens[s - 1], evens[s + 1]) for s in odds]
    received = swap_partner(payload, "seq")
    held = []
    for dist in range(reach + 1):
        held.append(evens[dist] if dist % 2 == 0 else received[(dist - 1) // 2])
    return held


def return_behind(parts, reach, paired, core):
    if not paired:
        carried = parts[reach]
        for dist in range(reach - 1, -1, -1):
            carried = shift_up(carried.astype(jnp.bfloat16), "seq", -1).astype(jnp.float32) + parts[dist]
        return carried
    odds = list(range(1, reach + 1, 2))
    received = swap_partner([parts[s] for s in odds], "seq")
    total = None
    for dist in range(0, reach + 2, 2):
        zero = jnp.zeros_like(parts[0])
        from_core1 = received[dist // 2] if dist // 2 < len(odds) else zero
        from_core0 = received[dist // 2 - 1] if dist >= 2 and dist // 2 - 1 < len(odds) else zero
        own = parts[dist] if dist <= reach else zero
        summed = own + jnp.where(core == 0, from_core1, from_core0)
        if dist == 0:
            total = summed
        else:
            total = total + shift_up(summed.astype(jnp.bfloat16), "seq", -dist).astype(jnp.float32)
    return total


def local(query_rows, key_rows, value_rows, out_grad, lengths, out_weight):
    seq_count = lax.axis_size("seq")
    device = lax.axis_index("seq")
    core = device % 2
    paired = seq_count % 2 == 0
    tok_rows = query_rows.shape[1]
    feature_width = query_rows.shape[2]
    total_frames = seq_count * tok_rows
    reach = min(-(-MOST // tok_rows), seq_count - 1)
    score_scale = HEAD_DIM ** (-0.5)
    utt_lengths = lengths[0]

    weight_cols = lax.all_gather(out_weight, "dp", axis=1, tiled=True)
    weight_full = lax.all_gather(weight_cols, "seq", axis=0, tiled=True)

    query_heads = head_major(query_rows[0], tok_rows)
    own_kv = jnp.stack([head_major(key_rows[0], tok_rows), head_major(value_rows[0], tok_rows)])
    held = gather_behind(own_kv, reach, paired, core)

    query_utt, query_stretch = frame_labels(utt_lengths, device * tok_rows, tok_rows, total_frames)
    block_visible = []
    for dist in range(reach + 1):
        key_utt, key_stretch = frame_labels(
            utt_lengths, (device - dist) * tok_rows, tok_rows, total_frames
        )
        block_visible.append(
            (query_utt[:, None] == key_utt[None, :]) & (key_stretch[None, :] <= query_stretch[:, None])
        )

    block_scores = []
    top_score = None
    for dist in range(reach + 1):
        scores = (
            jnp.einsum("hqe,hke->hqk", query_heads, held[dist][0], preferred_element_type=jnp.float32)
            * score_scale
        )
        scores = jnp.where(block_visible[dist][None], scores, MASKED_SCORE)
        block_scores.append(scores)
        block_top = jnp.max(scores, axis=2)
        top_score = block_top if top_score is None else jnp.maximum(top_score, block_top)
    row_sum = None
    weighted = None
    for dist in range(reach + 1):
        expo_full = jnp.where(
            block_visible[dist][None], jnp.exp(block_scores[dist] - top_score[:, :, None]), 0.0
        )
        part_sum = jnp.sum(expo_full, axis=2)
        product = jnp.einsum(
            "hqk,hke->hqe",
            expo_full.astype(jnp.bfloat16),
            held[dist][1],
            preferred_element_type=jnp.float32,
        )
        row_sum = part_sum if row_sum is None else row_sum + part_sum
        weighted = product if weighted is None else weighted + product
    attended_heads = (weighted / row_sum[:, :, None]).astype(jnp.bfloat16)
    attended = row_major(attended_heads, tok_rows)
    log_sum = top_score + jnp.log(row_sum)

    mixed_out = jnp.dot(attended, weight_full, preferred_element_type=jnp.float32).astype(
        jnp.bfloat16
    )
    upstream = out_grad[0]
    att_grad = lax.dot_general(
        upstream, weight_full, (((1,), (1,)), ((), ())), preferred_element_type=jnp.float32
    ).astype(jnp.bfloat16)

    partial_weight = lax.dot_general(
        attended, upstream, (((0,), (0,)), ((), ())), preferred_element_type=jnp.float32
    )
    seq_bits = max(seq_count.bit_length() - 1, 1)
    row_share = halving_scatter(
        partial_weight, "seq", 0, [step > 0 for step in range(seq_bits)]
    )
    weight_grad = halving_scatter(row_share, "dp", 1, [False] * 8)

    grad_heads = head_major(att_grad, tok_rows)
    delta_rows = jnp.sum(
        grad_heads.astype(jnp.float32) * attended_heads.astype(jnp.float32), axis=2
    )

    query_acc = None
    parts = [None] * (reach + 1)
    order = [d for d in range(reach, -1, -1) if d % 2 == 1] + [
        d for d in range(reach, -1, -1) if d % 2 == 0
    ]
    for dist in order:
        key_block = held[dist][0]
        value_block = held[dist][1]
        scores = (
            jnp.einsum("hqe,hke->hqk", query_heads, key_block, preferred_element_type=jnp.float32)
            * score_scale
        )
        prob_full = jnp.where(
            block_visible[dist][None], jnp.exp(scores - log_sum[:, :, None]), 0.0
        )
        prob_back = prob_full.astype(jnp.bfloat16)
        prob_grad = jnp.einsum(
            "hqe,hke->hqk", grad_heads, value_block, preferred_element_type=jnp.float32
        )
        score_grad = (prob_full * (prob_grad - delta_rows[:, :, None])).astype(jnp.bfloat16)
        query_part = jnp.einsum(
            "hqk,hke->hqe", score_grad, key_block, preferred_element_type=jnp.float32
        )
        query_acc = query_part if query_acc is None else query_acc + query_part
        key_part = (
            jnp.einsum("hqk,hqe->hke", score_grad, query_heads, preferred_element_type=jnp.float32)
            * score_scale
        )
        value_part = jnp.einsum(
            "hqk,hqe->hke", prob_back, grad_heads, preferred_element_type=jnp.float32
        )
        parts[dist] = jnp.stack([key_part, value_part])

    kv_grad = return_behind(parts, reach, paired, core)
    query_grad = row_major(query_acc * score_scale, tok_rows).astype(jnp.bfloat16)
    key_grad = row_major(kv_grad[0], tok_rows).astype(jnp.bfloat16)
    value_grad = row_major(kv_grad[1], tok_rows).astype(jnp.bfloat16)
    return (mixed_out[None], query_grad[None], key_grad[None], value_grad[None], weight_grad)


def solution(mesh):
    return jax.shard_map(
        local,
        mesh=mesh,
        in_specs=(
            P("dp", "seq", None),
            P("dp", "seq", None),
            P("dp", "seq", None),
            P("dp", "seq", None),
            P("dp", None),
            P("seq", "dp"),
        ),
        out_specs=(
            P("dp", "seq", None),
            P("dp", "seq", None),
            P("dp", "seq", None),
            P("dp", "seq", None),
            P("seq", "dp"),
        ),
        check_vma=False,
    )
```

```python
import jax
import jax.numpy as jnp
from jax import lax
from jax.sharding import PartitionSpec as P

HEADS = 12
HEAD_DIM = 64
STRETCH = 128
MOST = 1024


MASKED_SCORE = -1e30


def shift_up(block, axis, distance):
    devices = range(lax.axis_size(axis))
    route = [(i - distance, i) for i in devices if i - distance in devices]
    return lax.ppermute(block, axis, route)


def swap_partner(block, axis):
    count = lax.axis_size(axis)
    return lax.ppermute(block, axis, [(i, i ^ 1) for i in range(count)])


def halving_scatter(total, axis, dim, sends_narrow):
    count = lax.axis_size(axis)
    if count & (count - 1):
        return lax.psum_scatter(total, axis, scatter_dimension=dim, tiled=True)
    me = lax.axis_index(axis)
    bits = count.bit_length() - 1
    moved = jnp.moveaxis(total, dim, 0)
    rest = moved.shape[1:]
    blocks = moved.reshape((2,) * bits + (moved.shape[0] // count,) + rest)
    for step in range(bits):
        own_bit = (me >> step) % 2
        keep = lax.dynamic_index_in_dim(blocks, own_bit, blocks.ndim - len(rest) - 2, keepdims=False)
        give = lax.dynamic_index_in_dim(blocks, 1 - own_bit, blocks.ndim - len(rest) - 2, keepdims=False)
        if sends_narrow[step]:
            give = give.astype(jnp.bfloat16)
        got = lax.ppermute(give, axis, [(i, i ^ (1 << step)) for i in range(count)])
        blocks = keep + got.astype(keep.dtype)
    return jnp.moveaxis(blocks, 0, dim)


def frame_labels(utt_lengths, first_frame, frame_count, total_frames):
    positions = first_frame + jnp.arange(frame_count, dtype=jnp.int32)
    utt_ends = jnp.cumsum(utt_lengths)
    utt_index = jnp.sum((positions[:, None] >= utt_ends[None, :]).astype(jnp.int32), axis=1)
    outside = (positions < 0) | (positions >= total_frames)
    return (jnp.where(outside, -1, utt_index), positions // STRETCH)


def head_major(rows, tok_rows):
    return jnp.transpose(rows.reshape(tok_rows, HEADS, HEAD_DIM), (1, 0, 2))


def row_major(heads, tok_rows):
    return jnp.transpose(heads, (1, 0, 2)).reshape(tok_rows, HEADS * HEAD_DIM)


def gather_behind(own, reach, paired, core):
    if not paired:
        held = [own]
        for _ in range(reach):
            held.append(shift_up(held[-1], "seq", 1))
        return held
    evens = {0: own}
    for dist in range(2, reach + 2, 2):
        evens[dist] = shift_up(own, "seq", dist)
    odds = list(range(1, reach + 1, 2))
    payload = [jnp.where(core == 0, evens[s - 1], evens[s + 1]) for s in odds]
    received = swap_partner(payload, "seq")
    held = []
    for dist in range(reach + 1):
        held.append(evens[dist] if dist % 2 == 0 else received[(dist - 1) // 2])
    return held


def return_behind(parts, reach, paired, core):
    if not paired:
        carried = parts[reach]
        for dist in range(reach - 1, -1, -1):
            carried = shift_up(carried.astype(jnp.bfloat16), "seq", -1).astype(jnp.float32) + parts[dist]
        return carried
    odds = list(range(1, reach + 1, 2))
    received = swap_partner([parts[s] for s in odds], "seq")
    total = None
    for dist in range(0, reach + 2, 2):
        zero = jnp.zeros_like(parts[0])
        from_core1 = received[dist // 2] if dist // 2 < len(odds) else zero
        from_core0 = received[dist // 2 - 1] if dist >= 2 and dist // 2 - 1 < len(odds) else zero
        own = parts[dist] if dist <= reach else zero
        summed = own + jnp.where(core == 0, from_core1, from_core0)
        if dist == 0:
            total = summed
        else:
            total = total + shift_up(summed.astype(jnp.bfloat16), "seq", -dist).astype(jnp.float32)
    return total


def local(query_rows, key_rows, value_rows, out_grad, lengths, out_weight):
    seq_count = lax.axis_size("seq")
    device = lax.axis_index("seq")
    core = device % 2
    paired = seq_count % 2 == 0
    tok_rows = query_rows.shape[1]
    feature_width = query_rows.shape[2]
    total_frames = seq_count * tok_rows
    reach = min(-(-MOST // tok_rows), seq_count - 1)
    score_scale = HEAD_DIM ** (-0.5)
    utt_lengths = lengths[0]

    weight_cols = lax.all_gather(out_weight, "dp", axis=1, tiled=True)
    weight_full = lax.all_gather(weight_cols, "seq", axis=0, tiled=True)

    query_heads = head_major(query_rows[0], tok_rows)
    own_kv = jnp.stack([head_major(key_rows[0], tok_rows), head_major(value_rows[0], tok_rows)])
    held = gather_behind(own_kv, reach, paired, core)

    query_utt, query_stretch = frame_labels(utt_lengths, device * tok_rows, tok_rows, total_frames)
    block_visible = []
    for dist in range(reach + 1):
        key_utt, key_stretch = frame_labels(
            utt_lengths, (device - dist) * tok_rows, tok_rows, total_frames
        )
        block_visible.append(
            (query_utt[:, None] == key_utt[None, :]) & (key_stretch[None, :] <= query_stretch[:, None])
        )

    block_scores = []
    top_score = None
    for dist in range(reach + 1):
        scores = (
            jnp.einsum("hqe,hke->hqk", query_heads, held[dist][0], preferred_element_type=jnp.float32)
            * score_scale
        )
        scores = jnp.where(block_visible[dist][None], scores, MASKED_SCORE)
        block_scores.append(scores)
        block_top = jnp.max(scores, axis=2)
        top_score = block_top if top_score is None else jnp.maximum(top_score, block_top)
    row_sum = None
    weighted = None
    for dist in range(reach + 1):
        expo_full = jnp.where(
            block_visible[dist][None], jnp.exp(block_scores[dist] - top_score[:, :, None]), 0.0
        )
        part_sum = jnp.sum(expo_full, axis=2)
        product = jnp.einsum(
            "hqk,hke->hqe",
            expo_full.astype(jnp.bfloat16),
            held[dist][1],
            preferred_element_type=jnp.float32,
        )
        row_sum = part_sum if row_sum is None else row_sum + part_sum
        weighted = product if weighted is None else weighted + product
    attended_heads = (weighted / row_sum[:, :, None]).astype(jnp.bfloat16)
    attended = row_major(attended_heads, tok_rows)
    log_sum = top_score + jnp.log(row_sum)

    mixed_out = jnp.dot(attended, weight_full, preferred_element_type=jnp.float32).astype(
        jnp.bfloat16
    )
    upstream = out_grad[0]
    att_grad = lax.dot_general(
        upstream, weight_full, (((1,), (1,)), ((), ())), preferred_element_type=jnp.float32
    ).astype(jnp.bfloat16)

    partial_weight = lax.dot_general(
        attended, upstream, (((0,), (0,)), ((), ())), preferred_element_type=jnp.float32
    )
    col_share = halving_scatter(partial_weight, "dp", 1, [False] * 8)
    weight_grad = lax.psum_scatter(
        col_share.astype(jnp.bfloat16), "seq", scatter_dimension=0, tiled=True
    ).astype(jnp.float32)

    grad_heads = head_major(att_grad, tok_rows)
    delta_rows = jnp.sum(
        grad_heads.astype(jnp.float32) * attended_heads.astype(jnp.float32), axis=2
    )

    query_acc = None
    parts = [None] * (reach + 1)
    order = [d for d in range(reach, -1, -1) if d % 2 == 1] + [
        d for d in range(reach, -1, -1) if d % 2 == 0
    ]
    for dist in order:
        key_block = held[dist][0]
        value_block = held[dist][1]
        scores = (
            jnp.einsum("hqe,hke->hqk", query_heads, key_block, preferred_element_type=jnp.float32)
            * score_scale
        )
        prob_full = jnp.where(
            block_visible[dist][None], jnp.exp(scores - log_sum[:, :, None]), 0.0
        )
        prob_back = prob_full.astype(jnp.bfloat16)
        prob_grad = jnp.einsum(
            "hqe,hke->hqk", grad_heads, value_block, preferred_element_type=jnp.float32
        )
        score_grad = (prob_full * (prob_grad - delta_rows[:, :, None])).astype(jnp.bfloat16)
        query_part = jnp.einsum(
            "hqk,hke->hqe", score_grad, key_block, preferred_element_type=jnp.float32
        )
        query_acc = query_part if query_acc is None else query_acc + query_part
        key_part = (
            jnp.einsum("hqk,hqe->hke", score_grad, query_heads, preferred_element_type=jnp.float32)
            * score_scale
        )
        value_part = jnp.einsum(
            "hqk,hqe->hke", prob_back, grad_heads, preferred_element_type=jnp.float32
        )
        parts[dist] = jnp.stack([key_part, value_part])

    kv_grad = return_behind(parts, reach, paired, core)
    query_grad = row_major(query_acc * score_scale, tok_rows).astype(jnp.bfloat16)
    key_grad = row_major(kv_grad[0], tok_rows).astype(jnp.bfloat16)
    value_grad = row_major(kv_grad[1], tok_rows).astype(jnp.bfloat16)
    return (mixed_out[None], query_grad[None], key_grad[None], value_grad[None], weight_grad)


def solution(mesh):
    return jax.shard_map(
        local,
        mesh=mesh,
        in_specs=(
            P("dp", "seq", None),
            P("dp", "seq", None),
            P("dp", "seq", None),
            P("dp", "seq", None),
            P("dp", None),
            P("seq", "dp"),
        ),
        out_specs=(
            P("dp", "seq", None),
            P("dp", "seq", None),
            P("dp", "seq", None),
            P("dp", "seq", None),
            P("seq", "dp"),
        ),
        check_vma=False,
    )
```

```python
import jax
import jax.numpy as jnp
from jax import lax
from jax.sharding import PartitionSpec as P

HEADS = 12
HEAD_DIM = 64
STRETCH = 128
MOST = 1024


MASKED_SCORE = -1e30


SEQ = ("chip", "core")


def axis_count(axis):
    if isinstance(axis, tuple):
        count = 1
        for name in axis:
            count *= lax.axis_size(name)
        return count
    return lax.axis_size(axis)


def shift_up(block, axis, distance):
    devices = range(axis_count(axis))
    route = [(i - distance, i) for i in devices if i - distance in devices]
    return lax.ppermute(block, axis, route)


def swap_partner(block, axis):
    return lax.ppermute(block, "core", [(0, 1), (1, 0)])


def frame_labels(utt_lengths, first_frame, frame_count, total_frames):
    positions = first_frame + jnp.arange(frame_count, dtype=jnp.int32)
    utt_ends = jnp.cumsum(utt_lengths)
    utt_index = jnp.sum((positions[:, None] >= utt_ends[None, :]).astype(jnp.int32), axis=1)
    outside = (positions < 0) | (positions >= total_frames)
    return (jnp.where(outside, -1, utt_index), positions // STRETCH)


def head_major(rows, tok_rows):
    return jnp.transpose(rows.reshape(tok_rows, HEADS, HEAD_DIM), (1, 0, 2))


def row_major(heads, tok_rows):
    return jnp.transpose(heads, (1, 0, 2)).reshape(tok_rows, HEADS * HEAD_DIM)


def gather_behind(own, reach, paired, core):
    if not paired:
        held = [own]
        for _ in range(reach):
            held.append(shift_up(held[-1], SEQ, 1))
        return held
    evens = {0: own}
    for dist in range(2, reach + 2, 2):
        evens[dist] = shift_up(own, SEQ, dist)
    odds = list(range(1, reach + 1, 2))
    payload = [jnp.where(core == 0, evens[s - 1], evens[s + 1]) for s in odds]
    received = swap_partner(payload, SEQ)
    held = []
    for dist in range(reach + 1):
        held.append(evens[dist] if dist % 2 == 0 else received[(dist - 1) // 2])
    return held


def return_behind(parts, reach, paired, core):
    if not paired:
        carried = parts[reach]
        for dist in range(reach - 1, -1, -1):
            carried = shift_up(carried.astype(jnp.bfloat16), SEQ, -1).astype(jnp.float32) + parts[dist]
        return carried
    odds = list(range(1, reach + 1, 2))
    received = swap_partner([parts[s] for s in odds], SEQ)
    total = None
    for dist in range(0, reach + 2, 2):
        zero = jnp.zeros_like(parts[0])
        from_core1 = received[dist // 2] if dist // 2 < len(odds) else zero
        from_core0 = received[dist // 2 - 1] if dist >= 2 and dist // 2 - 1 < len(odds) else zero
        own = parts[dist] if dist <= reach else zero
        summed = own + jnp.where(core == 0, from_core1, from_core0)
        if dist == 0:
            total = summed
        else:
            total = total + shift_up(summed.astype(jnp.bfloat16), SEQ, -dist).astype(jnp.float32)
    return total


def local(query_rows, key_rows, value_rows, out_grad, lengths, out_weight):
    seq_count = axis_count(SEQ)
    device = lax.axis_index(SEQ)
    core = lax.axis_index("core")
    paired = True
    tok_rows = query_rows.shape[1]
    feature_width = query_rows.shape[2]
    total_frames = seq_count * tok_rows
    reach = min(-(-MOST // tok_rows), seq_count - 1)
    score_scale = HEAD_DIM ** (-0.5)
    utt_lengths = lengths[0]

    weight_cols = lax.all_gather(out_weight, "dp", axis=1, tiled=True)
    weight_full = lax.all_gather(weight_cols, SEQ, axis=0, tiled=True)

    query_heads = head_major(query_rows[0], tok_rows)
    own_kv = jnp.stack([head_major(key_rows[0], tok_rows), head_major(value_rows[0], tok_rows)])
    held = gather_behind(own_kv, reach, paired, core)

    query_utt, query_stretch = frame_labels(utt_lengths, device * tok_rows, tok_rows, total_frames)
    block_visible = []
    for dist in range(reach + 1):
        key_utt, key_stretch = frame_labels(
            utt_lengths, (device - dist) * tok_rows, tok_rows, total_frames
        )
        block_visible.append(
            (query_utt[:, None] == key_utt[None, :]) & (key_stretch[None, :] <= query_stretch[:, None])
        )

    block_scores = []
    top_score = None
    for dist in range(reach + 1):
        scores = (
            jnp.einsum("hqe,hke->hqk", query_heads, held[dist][0], preferred_element_type=jnp.float32)
            * score_scale
        )
        scores = jnp.where(block_visible[dist][None], scores, MASKED_SCORE)
        block_scores.append(scores)
        block_top = jnp.max(scores, axis=2)
        top_score = block_top if top_score is None else jnp.maximum(top_score, block_top)
    row_sum = None
    weighted = None
    for dist in range(reach + 1):
        expo_full = jnp.where(
            block_visible[dist][None], jnp.exp(block_scores[dist] - top_score[:, :, None]), 0.0
        )
        part_sum = jnp.sum(expo_full, axis=2)
        product = jnp.einsum(
            "hqk,hke->hqe",
            expo_full.astype(jnp.bfloat16),
            held[dist][1],
            preferred_element_type=jnp.float32,
        )
        row_sum = part_sum if row_sum is None else row_sum + part_sum
        weighted = product if weighted is None else weighted + product
    attended_heads = (weighted / row_sum[:, :, None]).astype(jnp.bfloat16)
    attended = row_major(attended_heads, tok_rows)
    log_sum = top_score + jnp.log(row_sum)

    mixed_out = jnp.dot(attended, weight_full, preferred_element_type=jnp.float32).astype(
        jnp.bfloat16
    )
    upstream = out_grad[0]
    att_grad = lax.dot_general(
        upstream, weight_full, (((1,), (1,)), ((), ())), preferred_element_type=jnp.float32
    ).astype(jnp.bfloat16)

    partial_weight = lax.dot_general(
        attended, upstream, (((0,), (0,)), ((), ())), preferred_element_type=jnp.float32
    )
    chip_count = lax.axis_size("chip")
    halves = partial_weight.reshape(chip_count, 2, -1, partial_weight.shape[1])
    keep = lax.dynamic_index_in_dim(halves, core, 1, keepdims=False)
    give = lax.dynamic_index_in_dim(halves, 1 - core, 1, keepdims=False)
    core_sum = keep + swap_partner(give, SEQ)
    row_share = lax.psum_scatter(
        core_sum.reshape(-1, partial_weight.shape[1]).astype(jnp.bfloat16),
        "chip",
        scatter_dimension=0,
        tiled=True,
    )
    weight_grad = lax.psum_scatter(
        row_share.astype(jnp.float32), "dp", scatter_dimension=1, tiled=True
    )

    grad_heads = head_major(att_grad, tok_rows)
    delta_rows = jnp.sum(
        grad_heads.astype(jnp.float32) * attended_heads.astype(jnp.float32), axis=2
    )

    query_acc = None
    parts = [None] * (reach + 1)
    order = [d for d in range(reach, -1, -1) if d % 2 == 1] + [
        d for d in range(reach, -1, -1) if d % 2 == 0
    ]
    for dist in order:
        key_block = held[dist][0]
        value_block = held[dist][1]
        scores = (
            jnp.einsum("hqe,hke->hqk", query_heads, key_block, preferred_element_type=jnp.float32)
            * score_scale
        )
        prob_full = jnp.where(
            block_visible[dist][None], jnp.exp(scores - log_sum[:, :, None]), 0.0
        )
        prob_back = prob_full.astype(jnp.bfloat16)
        prob_grad = jnp.einsum(
            "hqe,hke->hqk", grad_heads, value_block, preferred_element_type=jnp.float32
        )
        score_grad = (prob_full * (prob_grad - delta_rows[:, :, None])).astype(jnp.bfloat16)
        query_part = jnp.einsum(
            "hqk,hke->hqe", score_grad, key_block, preferred_element_type=jnp.float32
        )
        query_acc = query_part if query_acc is None else query_acc + query_part
        key_part = (
            jnp.einsum("hqk,hqe->hke", score_grad, query_heads, preferred_element_type=jnp.float32)
            * score_scale
        )
        value_part = jnp.einsum(
            "hqk,hqe->hke", prob_back, grad_heads, preferred_element_type=jnp.float32
        )
        parts[dist] = jnp.stack([key_part, value_part])

    kv_grad = return_behind(parts, reach, paired, core)
    query_grad = row_major(query_acc * score_scale, tok_rows).astype(jnp.bfloat16)
    key_grad = row_major(kv_grad[0], tok_rows).astype(jnp.bfloat16)
    value_grad = row_major(kv_grad[1], tok_rows).astype(jnp.bfloat16)
    return (mixed_out[None], query_grad[None], key_grad[None], value_grad[None], weight_grad)


def solution(mesh):
    names = list(mesh.axis_names)
    at = names.index("seq")
    shape = mesh.devices.shape
    split_mesh = jax.sharding.Mesh(
        mesh.devices.reshape(shape[:at] + (shape[at] // 2, 2) + shape[at + 1 :]),
        tuple(names[:at] + ["chip", "core"] + names[at + 1 :]),
    )
    return jax.shard_map(
        local,
        mesh=split_mesh,
        in_specs=(
            P("dp", SEQ, None),
            P("dp", SEQ, None),
            P("dp", SEQ, None),
            P("dp", SEQ, None),
            P("dp", None),
            P(SEQ, "dp"),
        ),
        out_specs=(
            P("dp", SEQ, None),
            P("dp", SEQ, None),
            P("dp", SEQ, None),
            P("dp", SEQ, None),
            P(SEQ, "dp"),
        ),
        check_vma=False,
    )
```

```python
import jax
import jax.numpy as jnp
from jax import lax
from jax.sharding import PartitionSpec as P

HEADS = 12
HEAD_DIM = 64
STRETCH = 128
MOST = 1024


MASKED_SCORE = -1e30


def shift_up(block, axis, distance):
    devices = range(lax.axis_size(axis))
    route = [(i - distance, i) for i in devices if i - distance in devices]
    return lax.ppermute(block, axis, route)


def swap_partner(block, axis):
    count = lax.axis_size(axis)
    return lax.ppermute(block, axis, [(i, i ^ 1) for i in range(count)])


def halving_scatter(total, axis, dim, sends_narrow):
    count = lax.axis_size(axis)
    if count & (count - 1):
        return lax.psum_scatter(total, axis, scatter_dimension=dim, tiled=True)
    me = lax.axis_index(axis)
    bits = count.bit_length() - 1
    moved = jnp.moveaxis(total, dim, 0)
    rest = moved.shape[1:]
    blocks = moved.reshape((2,) * bits + (moved.shape[0] // count,) + rest)
    for step in range(bits):
        own_bit = (me >> step) % 2
        keep = lax.dynamic_index_in_dim(blocks, own_bit, blocks.ndim - len(rest) - 2, keepdims=False)
        give = lax.dynamic_index_in_dim(blocks, 1 - own_bit, blocks.ndim - len(rest) - 2, keepdims=False)
        if sends_narrow[step]:
            give = give.astype(jnp.bfloat16)
        got = lax.ppermute(give, axis, [(i, i ^ (1 << step)) for i in range(count)])
        blocks = keep + got.astype(keep.dtype)
    return jnp.moveaxis(blocks, 0, dim)


def frame_labels(utt_lengths, first_frame, frame_count, total_frames):
    positions = first_frame + jnp.arange(frame_count, dtype=jnp.int32)
    utt_ends = jnp.cumsum(utt_lengths)
    utt_index = jnp.sum((positions[:, None] >= utt_ends[None, :]).astype(jnp.int32), axis=1)
    outside = (positions < 0) | (positions >= total_frames)
    return (jnp.where(outside, -1, utt_index), positions // STRETCH)


def head_major(rows, tok_rows):
    return jnp.transpose(rows.reshape(tok_rows, HEADS, HEAD_DIM), (1, 0, 2))


def row_major(heads, tok_rows):
    return jnp.transpose(heads, (1, 0, 2)).reshape(tok_rows, HEADS * HEAD_DIM)


def gather_behind(own, reach, paired, core):
    if not paired:
        held = [own]
        for _ in range(reach):
            held.append(shift_up(held[-1], "seq", 1))
        return held
    evens = {0: own}
    for dist in range(2, reach + 2, 2):
        evens[dist] = shift_up(own, "seq", dist)
    odds = list(range(1, reach + 1, 2))
    payload = [jnp.where(core == 0, evens[s - 1], evens[s + 1]) for s in odds]
    received = swap_partner(payload, "seq")
    held = []
    for dist in range(reach + 1):
        held.append(evens[dist] if dist % 2 == 0 else received[(dist - 1) // 2])
    return held


def return_behind(parts, reach, paired, core):
    if not paired:
        carried = parts[reach]
        for dist in range(reach - 1, -1, -1):
            carried = shift_up(carried.astype(jnp.bfloat16), "seq", -1).astype(jnp.float32) + parts[dist]
        return carried
    odds = list(range(1, reach + 1, 2))
    received = swap_partner([parts[s] for s in odds], "seq")
    total = None
    for dist in range(0, reach + 2, 2):
        zero = jnp.zeros_like(parts[0])
        from_core1 = received[dist // 2] if dist // 2 < len(odds) else zero
        from_core0 = received[dist // 2 - 1] if dist >= 2 and dist // 2 - 1 < len(odds) else zero
        own = parts[dist] if dist <= reach else zero
        summed = own + jnp.where(core == 0, from_core1, from_core0)
        if dist == 0:
            total = summed
        else:
            total = total + shift_up(summed.astype(jnp.bfloat16), "seq", -dist).astype(jnp.float32)
    return total


def local(query_rows, key_rows, value_rows, out_grad, lengths, out_weight):
    seq_count = lax.axis_size("seq")
    device = lax.axis_index("seq")
    core = device % 2
    paired = seq_count % 2 == 0
    tok_rows = query_rows.shape[1]
    feature_width = query_rows.shape[2]
    total_frames = seq_count * tok_rows
    reach = min(-(-MOST // tok_rows), seq_count - 1)
    score_scale = HEAD_DIM ** (-0.5)
    utt_lengths = lengths[0]

    weight_cols = lax.all_gather(out_weight, "dp", axis=1, tiled=True)
    weight_full = lax.all_gather(weight_cols, "seq", axis=0, tiled=True)

    query_heads = head_major(query_rows[0], tok_rows)
    own_kv = jnp.stack([head_major(key_rows[0], tok_rows), head_major(value_rows[0], tok_rows)])
    held = gather_behind(own_kv, reach, paired, core)

    query_utt, query_stretch = frame_labels(utt_lengths, device * tok_rows, tok_rows, total_frames)
    block_visible = []
    for dist in range(reach + 1):
        key_utt, key_stretch = frame_labels(
            utt_lengths, (device - dist) * tok_rows, tok_rows, total_frames
        )
        block_visible.append(
            (query_utt[:, None] == key_utt[None, :]) & (key_stretch[None, :] <= query_stretch[:, None])
        )

    block_scores = []
    top_score = None
    for dist in range(reach + 1):
        scores = (
            jnp.einsum("hqe,hke->hqk", query_heads, held[dist][0], preferred_element_type=jnp.float32)
            * score_scale
        )
        scores = jnp.where(block_visible[dist][None], scores, MASKED_SCORE)
        block_scores.append(scores)
        block_top = jnp.max(scores, axis=2)
        top_score = block_top if top_score is None else jnp.maximum(top_score, block_top)
    row_sum = None
    weighted = None
    for dist in range(reach + 1):
        expo_full = jnp.where(
            block_visible[dist][None], jnp.exp(block_scores[dist] - top_score[:, :, None]), 0.0
        )
        part_sum = jnp.sum(expo_full, axis=2)
        product = jnp.einsum(
            "hqk,hke->hqe",
            expo_full.astype(jnp.bfloat16),
            held[dist][1],
            preferred_element_type=jnp.float32,
        )
        row_sum = part_sum if row_sum is None else row_sum + part_sum
        weighted = product if weighted is None else weighted + product
    attended_heads = (weighted / row_sum[:, :, None]).astype(jnp.bfloat16)
    attended = row_major(attended_heads, tok_rows)
    log_sum = top_score + jnp.log(row_sum)

    mixed_out = jnp.dot(attended, weight_full, preferred_element_type=jnp.float32).astype(
        jnp.bfloat16
    )
    upstream = out_grad[0]
    att_grad = lax.dot_general(
        upstream, weight_full, (((1,), (1,)), ((), ())), preferred_element_type=jnp.float32
    ).astype(jnp.bfloat16)

    partial_weight = lax.dot_general(
        attended, upstream, (((0,), (0,)), ((), ())), preferred_element_type=jnp.float32
    )

    grad_heads = head_major(att_grad, tok_rows)
    delta_rows = jnp.sum(
        grad_heads.astype(jnp.float32) * attended_heads.astype(jnp.float32), axis=2
    )

    query_acc = None
    parts = [None] * (reach + 1)
    order = [d for d in range(reach, -1, -1) if d % 2 == 1] + [
        d for d in range(reach, -1, -1) if d % 2 == 0
    ]
    for dist in order:
        key_block = held[dist][0]
        value_block = held[dist][1]
        scores = (
            jnp.einsum("hqe,hke->hqk", query_heads, key_block, preferred_element_type=jnp.float32)
            * score_scale
        )
        prob_full = jnp.where(
            block_visible[dist][None], jnp.exp(scores - log_sum[:, :, None]), 0.0
        )
        prob_back = prob_full.astype(jnp.bfloat16)
        prob_grad = jnp.einsum(
            "hqe,hke->hqk", grad_heads, value_block, preferred_element_type=jnp.float32
        )
        score_grad = (prob_full * (prob_grad - delta_rows[:, :, None])).astype(jnp.bfloat16)
        query_part = jnp.einsum(
            "hqk,hke->hqe", score_grad, key_block, preferred_element_type=jnp.float32
        )
        query_acc = query_part if query_acc is None else query_acc + query_part
        key_part = (
            jnp.einsum("hqk,hqe->hke", score_grad, query_heads, preferred_element_type=jnp.float32)
            * score_scale
        )
        value_part = jnp.einsum(
            "hqk,hqe->hke", prob_back, grad_heads, preferred_element_type=jnp.float32
        )
        parts[dist] = jnp.stack([key_part, value_part])

    partial_weight, parts = lax.optimization_barrier((partial_weight, parts))
    kv_grad = return_behind(parts, reach, paired, core)
    seq_bits = max(seq_count.bit_length() - 1, 1)
    row_share = halving_scatter(
        partial_weight, "seq", 0, [step > 0 for step in range(seq_bits)]
    )
    weight_grad = halving_scatter(row_share, "dp", 1, [False] * 8)
    query_grad = row_major(query_acc * score_scale, tok_rows).astype(jnp.bfloat16)
    key_grad = row_major(kv_grad[0], tok_rows).astype(jnp.bfloat16)
    value_grad = row_major(kv_grad[1], tok_rows).astype(jnp.bfloat16)
    return (mixed_out[None], query_grad[None], key_grad[None], value_grad[None], weight_grad)


def solution(mesh):
    return jax.shard_map(
        local,
        mesh=mesh,
        in_specs=(
            P("dp", "seq", None),
            P("dp", "seq", None),
            P("dp", "seq", None),
            P("dp", "seq", None),
            P("dp", None),
            P("seq", "dp"),
        ),
        out_specs=(
            P("dp", "seq", None),
            P("dp", "seq", None),
            P("dp", "seq", None),
            P("dp", "seq", None),
            P("seq", "dp"),
        ),
        check_vma=False,
    )
```

```python
import jax
import jax.numpy as jnp
from jax import lax
from jax.sharding import PartitionSpec as P

HEADS = 12
HEAD_DIM = 64
STRETCH = 128
MOST = 1024


MASKED_SCORE = -1e30


SEQ = ("zc", "yc", "core")


def axis_count(axis):
    if isinstance(axis, tuple):
        count = 1
        for name in axis:
            count *= lax.axis_size(name)
        return count
    return lax.axis_size(axis)


def shift_up(block, axis, distance):
    devices = range(axis_count(axis))
    route = [(i - distance, i) for i in devices if i - distance in devices]
    return lax.ppermute(block, axis, route)


def swap_partner(block, axis):
    return lax.ppermute(block, "core", [(0, 1), (1, 0)])


def frame_labels(utt_lengths, first_frame, frame_count, total_frames):
    positions = first_frame + jnp.arange(frame_count, dtype=jnp.int32)
    utt_ends = jnp.cumsum(utt_lengths)
    utt_index = jnp.sum((positions[:, None] >= utt_ends[None, :]).astype(jnp.int32), axis=1)
    outside = (positions < 0) | (positions >= total_frames)
    return (jnp.where(outside, -1, utt_index), positions // STRETCH)


def head_major(rows, tok_rows):
    return jnp.transpose(rows.reshape(tok_rows, HEADS, HEAD_DIM), (1, 0, 2))


def row_major(heads, tok_rows):
    return jnp.transpose(heads, (1, 0, 2)).reshape(tok_rows, HEADS * HEAD_DIM)


def gather_behind(own, reach, paired, core):
    if not paired:
        held = [own]
        for _ in range(reach):
            held.append(shift_up(held[-1], SEQ, 1))
        return held
    evens = {0: own}
    for dist in range(2, reach + 2, 2):
        evens[dist] = shift_up(own, SEQ, dist)
    odds = list(range(1, reach + 1, 2))
    payload = [jnp.where(core == 0, evens[s - 1], evens[s + 1]) for s in odds]
    received = swap_partner(payload, SEQ)
    held = []
    for dist in range(reach + 1):
        held.append(evens[dist] if dist % 2 == 0 else received[(dist - 1) // 2])
    return held


def return_behind(parts, reach, paired, core):
    if not paired:
        carried = parts[reach]
        for dist in range(reach - 1, -1, -1):
            carried = shift_up(carried.astype(jnp.bfloat16), SEQ, -1).astype(jnp.float32) + parts[dist]
        return carried
    odds = list(range(1, reach + 1, 2))
    received = swap_partner([parts[s] for s in odds], SEQ)
    total = None
    for dist in range(0, reach + 2, 2):
        zero = jnp.zeros_like(parts[0])
        from_core1 = received[dist // 2] if dist // 2 < len(odds) else zero
        from_core0 = received[dist // 2 - 1] if dist >= 2 and dist // 2 - 1 < len(odds) else zero
        own = parts[dist] if dist <= reach else zero
        summed = own + jnp.where(core == 0, from_core1, from_core0)
        if dist == 0:
            total = summed
        else:
            total = total + shift_up(summed.astype(jnp.bfloat16), SEQ, -dist).astype(jnp.float32)
    return total


def local(query_rows, key_rows, value_rows, out_grad, lengths, out_weight):
    seq_count = axis_count(SEQ)
    device = lax.axis_index(SEQ)
    core = lax.axis_index("core")
    paired = True
    tok_rows = query_rows.shape[1]
    feature_width = query_rows.shape[2]
    total_frames = seq_count * tok_rows
    reach = min(-(-MOST // tok_rows), seq_count - 1)
    score_scale = HEAD_DIM ** (-0.5)
    utt_lengths = lengths[0]

    weight_cols = lax.all_gather(out_weight, "dp", axis=1, tiled=True)
    weight_full = lax.all_gather(weight_cols, SEQ, axis=0, tiled=True)

    query_heads = head_major(query_rows[0], tok_rows)
    own_kv = jnp.stack([head_major(key_rows[0], tok_rows), head_major(value_rows[0], tok_rows)])
    held = gather_behind(own_kv, reach, paired, core)

    query_utt, query_stretch = frame_labels(utt_lengths, device * tok_rows, tok_rows, total_frames)
    block_visible = []
    for dist in range(reach + 1):
        key_utt, key_stretch = frame_labels(
            utt_lengths, (device - dist) * tok_rows, tok_rows, total_frames
        )
        block_visible.append(
            (query_utt[:, None] == key_utt[None, :]) & (key_stretch[None, :] <= query_stretch[:, None])
        )

    block_scores = []
    top_score = None
    for dist in range(reach + 1):
        scores = (
            jnp.einsum("hqe,hke->hqk", query_heads, held[dist][0], preferred_element_type=jnp.float32)
            * score_scale
        )
        scores = jnp.where(block_visible[dist][None], scores, MASKED_SCORE)
        block_scores.append(scores)
        block_top = jnp.max(scores, axis=2)
        top_score = block_top if top_score is None else jnp.maximum(top_score, block_top)
    row_sum = None
    weighted = None
    for dist in range(reach + 1):
        expo_full = jnp.where(
            block_visible[dist][None], jnp.exp(block_scores[dist] - top_score[:, :, None]), 0.0
        )
        part_sum = jnp.sum(expo_full, axis=2)
        product = jnp.einsum(
            "hqk,hke->hqe",
            expo_full.astype(jnp.bfloat16),
            held[dist][1],
            preferred_element_type=jnp.float32,
        )
        row_sum = part_sum if row_sum is None else row_sum + part_sum
        weighted = product if weighted is None else weighted + product
    attended_heads = (weighted / row_sum[:, :, None]).astype(jnp.bfloat16)
    attended = row_major(attended_heads, tok_rows)
    log_sum = top_score + jnp.log(row_sum)

    mixed_out = jnp.dot(attended, weight_full, preferred_element_type=jnp.float32).astype(
        jnp.bfloat16
    )
    upstream = out_grad[0]
    att_grad = lax.dot_general(
        upstream, weight_full, (((1,), (1,)), ((), ())), preferred_element_type=jnp.float32
    ).astype(jnp.bfloat16)

    partial_weight = lax.dot_general(
        attended, upstream, (((0,), (0,)), ((), ())), preferred_element_type=jnp.float32
    )
    columns = partial_weight.shape[1]
    quarters = partial_weight.reshape(lax.axis_size("zc"), 2, 2, -1, columns)
    keep = lax.dynamic_index_in_dim(quarters, core, 2, keepdims=False)
    give = lax.dynamic_index_in_dim(quarters, 1 - core, 2, keepdims=False)
    core_sum = keep + swap_partner(give, SEQ)
    row_pair = lax.axis_index("yc")
    keep = lax.dynamic_index_in_dim(core_sum, row_pair, 1, keepdims=False)
    give = lax.dynamic_index_in_dim(core_sum, 1 - row_pair, 1, keepdims=False)
    pair_sum = keep + lax.ppermute(give.astype(jnp.bfloat16), "yc", [(0, 1), (1, 0)]).astype(
        jnp.float32
    )
    row_share = lax.psum_scatter(
        pair_sum.reshape(-1, columns).astype(jnp.bfloat16),
        "zc",
        scatter_dimension=0,
        tiled=True,
    )
    weight_grad = lax.psum_scatter(
        row_share.astype(jnp.float32), "dp", scatter_dimension=1, tiled=True
    )

    grad_heads = head_major(att_grad, tok_rows)
    delta_rows = jnp.sum(
        grad_heads.astype(jnp.float32) * attended_heads.astype(jnp.float32), axis=2
    )

    query_acc = None
    parts = [None] * (reach + 1)
    order = [d for d in range(reach, -1, -1) if d % 2 == 1] + [
        d for d in range(reach, -1, -1) if d % 2 == 0
    ]
    for dist in order:
        key_block = held[dist][0]
        value_block = held[dist][1]
        scores = (
            jnp.einsum("hqe,hke->hqk", query_heads, key_block, preferred_element_type=jnp.float32)
            * score_scale
        )
        prob_full = jnp.where(
            block_visible[dist][None], jnp.exp(scores - log_sum[:, :, None]), 0.0
        )
        prob_back = prob_full.astype(jnp.bfloat16)
        prob_grad = jnp.einsum(
            "hqe,hke->hqk", grad_heads, value_block, preferred_element_type=jnp.float32
        )
        score_grad = (prob_full * (prob_grad - delta_rows[:, :, None])).astype(jnp.bfloat16)
        query_part = jnp.einsum(
            "hqk,hke->hqe", score_grad, key_block, preferred_element_type=jnp.float32
        )
        query_acc = query_part if query_acc is None else query_acc + query_part
        key_part = (
            jnp.einsum("hqk,hqe->hke", score_grad, query_heads, preferred_element_type=jnp.float32)
            * score_scale
        )
        value_part = jnp.einsum(
            "hqk,hqe->hke", prob_back, grad_heads, preferred_element_type=jnp.float32
        )
        parts[dist] = jnp.stack([key_part, value_part])

    kv_grad = return_behind(parts, reach, paired, core)
    query_grad = row_major(query_acc * score_scale, tok_rows).astype(jnp.bfloat16)
    key_grad = row_major(kv_grad[0], tok_rows).astype(jnp.bfloat16)
    value_grad = row_major(kv_grad[1], tok_rows).astype(jnp.bfloat16)
    return (mixed_out[None], query_grad[None], key_grad[None], value_grad[None], weight_grad)


def solution(mesh):
    names = list(mesh.axis_names)
    at = names.index("seq")
    shape = mesh.devices.shape
    split_mesh = jax.sharding.Mesh(
        mesh.devices.reshape(shape[:at] + (shape[at] // 4, 2, 2) + shape[at + 1 :]),
        tuple(names[:at] + ["zc", "yc", "core"] + names[at + 1 :]),
    )
    return jax.shard_map(
        local,
        mesh=split_mesh,
        in_specs=(
            P("dp", SEQ, None),
            P("dp", SEQ, None),
            P("dp", SEQ, None),
            P("dp", SEQ, None),
            P("dp", None),
            P(SEQ, "dp"),
        ),
        out_specs=(
            P("dp", SEQ, None),
            P("dp", SEQ, None),
            P("dp", SEQ, None),
            P("dp", SEQ, None),
            P(SEQ, "dp"),
        ),
        check_vma=False,
    )
```

```python
import jax
import jax.numpy as jnp
from jax import lax
from jax.sharding import PartitionSpec as P

HEADS = 12
HEAD_DIM = 64
STRETCH = 128
MOST = 1024


MASKED_SCORE = -1e30


SEQ = ("zc", "yc", "core")


def axis_count(axis):
    if isinstance(axis, tuple):
        count = 1
        for name in axis:
            count *= lax.axis_size(name)
        return count
    return lax.axis_size(axis)


def shift_up(block, axis, distance):
    devices = range(axis_count(axis))
    route = [(i - distance, i) for i in devices if i - distance in devices]
    return lax.ppermute(block, axis, route)


def swap_partner(block, axis):
    return lax.ppermute(block, "core", [(0, 1), (1, 0)])


def frame_labels(utt_lengths, first_frame, frame_count, total_frames):
    positions = first_frame + jnp.arange(frame_count, dtype=jnp.int32)
    utt_ends = jnp.cumsum(utt_lengths)
    utt_index = jnp.sum((positions[:, None] >= utt_ends[None, :]).astype(jnp.int32), axis=1)
    outside = (positions < 0) | (positions >= total_frames)
    return (jnp.where(outside, -1, utt_index), positions // STRETCH)


def head_major(rows, tok_rows):
    return jnp.transpose(rows.reshape(tok_rows, HEADS, HEAD_DIM), (1, 0, 2))


def row_major(heads, tok_rows):
    return jnp.transpose(heads, (1, 0, 2)).reshape(tok_rows, HEADS * HEAD_DIM)


def gather_behind(own, reach, paired, core):
    if not paired:
        held = [own]
        for _ in range(reach):
            held.append(shift_up(held[-1], SEQ, 1))
        return held
    evens = {0: own}
    for dist in range(2, reach + 2, 2):
        evens[dist] = shift_up(own, SEQ, dist)
    odds = list(range(1, reach + 1, 2))
    payload = [jnp.where(core == 0, evens[s - 1], evens[s + 1]) for s in odds]
    received = swap_partner(payload, SEQ)
    held = []
    for dist in range(reach + 1):
        held.append(evens[dist] if dist % 2 == 0 else received[(dist - 1) // 2])
    return held


def return_behind(parts, reach, paired, core):
    if not paired:
        carried = parts[reach]
        for dist in range(reach - 1, -1, -1):
            carried = shift_up(carried.astype(jnp.bfloat16), SEQ, -1).astype(jnp.float32) + parts[dist]
        return carried
    odds = list(range(1, reach + 1, 2))
    received = swap_partner([parts[s] for s in odds], SEQ)
    total = None
    for dist in range(0, reach + 2, 2):
        zero = jnp.zeros_like(parts[0])
        from_core1 = received[dist // 2] if dist // 2 < len(odds) else zero
        from_core0 = received[dist // 2 - 1] if dist >= 2 and dist // 2 - 1 < len(odds) else zero
        own = parts[dist] if dist <= reach else zero
        summed = own + jnp.where(core == 0, from_core1, from_core0)
        if dist == 0:
            total = summed
        else:
            total = total + shift_up(summed.astype(jnp.bfloat16), SEQ, -dist).astype(jnp.float32)
    return total


def local(query_rows, key_rows, value_rows, out_grad, lengths, out_weight):
    seq_count = axis_count(SEQ)
    device = lax.axis_index(SEQ)
    core = lax.axis_index("core")
    paired = True
    tok_rows = query_rows.shape[1]
    feature_width = query_rows.shape[2]
    total_frames = seq_count * tok_rows
    reach = min(-(-MOST // tok_rows), seq_count - 1)
    score_scale = HEAD_DIM ** (-0.5)
    utt_lengths = lengths[0]

    weight_cols = lax.all_gather(out_weight, "dp", axis=1, tiled=True)
    weight_full = lax.all_gather(weight_cols, SEQ, axis=0, tiled=True)

    query_heads = head_major(query_rows[0], tok_rows)
    own_kv = jnp.stack([head_major(key_rows[0], tok_rows), head_major(value_rows[0], tok_rows)])
    held = gather_behind(own_kv, reach, paired, core)

    query_utt, query_stretch = frame_labels(utt_lengths, device * tok_rows, tok_rows, total_frames)
    block_visible = []
    for dist in range(reach + 1):
        key_utt, key_stretch = frame_labels(
            utt_lengths, (device - dist) * tok_rows, tok_rows, total_frames
        )
        block_visible.append(
            (query_utt[:, None] == key_utt[None, :]) & (key_stretch[None, :] <= query_stretch[:, None])
        )

    block_scores = []
    top_score = None
    for dist in range(reach + 1):
        scores = (
            jnp.einsum("hqe,hke->hqk", query_heads, held[dist][0], preferred_element_type=jnp.float32)
            * score_scale
        )
        scores = jnp.where(block_visible[dist][None], scores, MASKED_SCORE)
        block_scores.append(scores)
        block_top = jnp.max(scores, axis=2)
        top_score = block_top if top_score is None else jnp.maximum(top_score, block_top)
    row_sum = None
    weighted = None
    for dist in range(reach + 1):
        expo_full = jnp.where(
            block_visible[dist][None], jnp.exp(block_scores[dist] - top_score[:, :, None]), 0.0
        )
        part_sum = jnp.sum(expo_full, axis=2)
        product = jnp.einsum(
            "hqk,hke->hqe",
            expo_full.astype(jnp.bfloat16),
            held[dist][1],
            preferred_element_type=jnp.float32,
        )
        row_sum = part_sum if row_sum is None else row_sum + part_sum
        weighted = product if weighted is None else weighted + product
    attended_heads = (weighted / row_sum[:, :, None]).astype(jnp.bfloat16)
    attended = row_major(attended_heads, tok_rows)
    log_sum = top_score + jnp.log(row_sum)

    mixed_out = jnp.dot(attended, weight_full, preferred_element_type=jnp.float32).astype(
        jnp.bfloat16
    )
    upstream = out_grad[0]
    att_grad = lax.dot_general(
        upstream, weight_full, (((1,), (1,)), ((), ())), preferred_element_type=jnp.float32
    ).astype(jnp.bfloat16)

    partial_weight = lax.dot_general(
        attended, upstream, (((0,), (0,)), ((), ())), preferred_element_type=jnp.float32
    )
    columns = partial_weight.shape[1]
    quarters = partial_weight.reshape(lax.axis_size("zc"), 2, 2, -1, columns)
    keep = lax.dynamic_index_in_dim(quarters, core, 2, keepdims=False)
    give = lax.dynamic_index_in_dim(quarters, 1 - core, 2, keepdims=False)
    core_sum = keep + swap_partner(give, SEQ)
    row_pair = lax.axis_index("yc")
    keep = lax.dynamic_index_in_dim(core_sum, row_pair, 1, keepdims=False)
    give = lax.dynamic_index_in_dim(core_sum, 1 - row_pair, 1, keepdims=False)
    pair_sum = keep + lax.ppermute(give.astype(jnp.bfloat16), "yc", [(0, 1), (1, 0)]).astype(
        jnp.float32
    )

    grad_heads = head_major(att_grad, tok_rows)
    delta_rows = jnp.sum(
        grad_heads.astype(jnp.float32) * attended_heads.astype(jnp.float32), axis=2
    )

    query_acc = None
    parts = [None] * (reach + 1)
    order = [d for d in range(reach, -1, -1) if d % 2 == 1] + [
        d for d in range(reach, -1, -1) if d % 2 == 0
    ]
    odds_first = [d for d in range(reach, -1, -1) if d % 2 == 1]
    for dist in order:
        key_block = held[dist][0]
        value_block = held[dist][1]
        scores = (
            jnp.einsum("hqe,hke->hqk", query_heads, key_block, preferred_element_type=jnp.float32)
            * score_scale
        )
        prob_full = jnp.where(
            block_visible[dist][None], jnp.exp(scores - log_sum[:, :, None]), 0.0
        )
        prob_back = prob_full.astype(jnp.bfloat16)
        prob_grad = jnp.einsum(
            "hqe,hke->hqk", grad_heads, value_block, preferred_element_type=jnp.float32
        )
        score_grad = (prob_full * (prob_grad - delta_rows[:, :, None])).astype(jnp.bfloat16)
        query_part = jnp.einsum(
            "hqk,hke->hqe", score_grad, key_block, preferred_element_type=jnp.float32
        )
        query_acc = query_part if query_acc is None else query_acc + query_part
        key_part = (
            jnp.einsum("hqk,hqe->hke", score_grad, query_heads, preferred_element_type=jnp.float32)
            * score_scale
        )
        value_part = jnp.einsum(
            "hqk,hqe->hke", prob_back, grad_heads, preferred_element_type=jnp.float32
        )
        parts[dist] = jnp.stack([key_part, value_part])
        if dist == odds_first[-1]:
            pair_sum, first_parts = lax.optimization_barrier(
                (pair_sum, [parts[d] for d in odds_first])
            )
            for d, p in zip(odds_first, first_parts):
                parts[d] = p

    row_share = lax.psum_scatter(
        pair_sum.reshape(-1, columns).astype(jnp.bfloat16),
        "zc",
        scatter_dimension=0,
        tiled=True,
    )
    weight_grad = lax.psum_scatter(
        row_share.astype(jnp.float32), "dp", scatter_dimension=1, tiled=True
    )
    kv_grad = return_behind(parts, reach, paired, core)
    query_grad = row_major(query_acc * score_scale, tok_rows).astype(jnp.bfloat16)
    key_grad = row_major(kv_grad[0], tok_rows).astype(jnp.bfloat16)
    value_grad = row_major(kv_grad[1], tok_rows).astype(jnp.bfloat16)
    return (mixed_out[None], query_grad[None], key_grad[None], value_grad[None], weight_grad)


def solution(mesh):
    names = list(mesh.axis_names)
    at = names.index("seq")
    shape = mesh.devices.shape
    split_mesh = jax.sharding.Mesh(
        mesh.devices.reshape(shape[:at] + (shape[at] // 4, 2, 2) + shape[at + 1 :]),
        tuple(names[:at] + ["zc", "yc", "core"] + names[at + 1 :]),
    )
    return jax.shard_map(
        local,
        mesh=split_mesh,
        in_specs=(
            P("dp", SEQ, None),
            P("dp", SEQ, None),
            P("dp", SEQ, None),
            P("dp", SEQ, None),
            P("dp", None),
            P(SEQ, "dp"),
        ),
        out_specs=(
            P("dp", SEQ, None),
            P("dp", SEQ, None),
            P("dp", SEQ, None),
            P("dp", SEQ, None),
            P(SEQ, "dp"),
        ),
        check_vma=False,
    )
```

```python
import jax
import jax.numpy as jnp
from jax import lax
from jax.sharding import PartitionSpec as P

HEADS = 12
HEAD_DIM = 64
STRETCH = 128
MOST = 1024


MASKED_SCORE = -1e30


def shift_up(block, axis, distance):
    devices = range(lax.axis_size(axis))
    route = [(i - distance, i) for i in devices if i - distance in devices]
    return lax.ppermute(block, axis, route)


def swap_partner(block, axis):
    count = lax.axis_size(axis)
    return lax.ppermute(block, axis, [(i, i ^ 1) for i in range(count)])


def frame_labels(utt_lengths, first_frame, frame_count, total_frames):
    positions = first_frame + jnp.arange(frame_count, dtype=jnp.int32)
    utt_ends = jnp.cumsum(utt_lengths)
    utt_index = jnp.sum((positions[:, None] >= utt_ends[None, :]).astype(jnp.int32), axis=1)
    outside = (positions < 0) | (positions >= total_frames)
    return (jnp.where(outside, -1, utt_index), positions // STRETCH)


def head_major(rows, tok_rows):
    return jnp.transpose(rows.reshape(tok_rows, HEADS, HEAD_DIM), (1, 0, 2))


def row_major(heads, tok_rows):
    return jnp.transpose(heads, (1, 0, 2)).reshape(tok_rows, HEADS * HEAD_DIM)


def gather_behind(own, reach, paired, core):
    if not paired:
        held = [own]
        for _ in range(reach):
            held.append(shift_up(held[-1], "seq", 1))
        return held
    evens = {0: own}
    count = lax.axis_size("seq")
    if reach == 4 and count % 4 == 0:
        row = (lax.axis_index("seq") // 2) % 2
        later = [i for i in range(count) if (i // 2) % 2 == 1]
        earlier = [i for i in range(count) if (i // 2) % 2 == 0 and i + 2 < count]
        far = [shift_up(own[k], "seq", 4) for k in range(2)]
        near = []
        for k in range(2):
            direct = lax.ppermute(own[k], "seq", [(i - 2, i) for i in later])
            relayed = lax.ppermute(far[k], "seq", [(i + 2, i) for i in earlier])
            near.append(jnp.where(row == 1, direct, relayed))
        evens[2] = jnp.stack(near)
        evens[4] = jnp.stack(far)
    else:
        for dist in range(2, reach + 2, 2):
            evens[dist] = shift_up(own, "seq", dist)
    odds = list(range(1, reach + 1, 2))
    payload = [jnp.where(core == 0, evens[s - 1], evens[s + 1]) for s in odds]
    received = swap_partner(payload, "seq")
    held = []
    for dist in range(reach + 1):
        held.append(evens[dist] if dist % 2 == 0 else received[(dist - 1) // 2])
    return held


def return_behind(parts, reach, paired, core):
    if not paired:
        carried = parts[reach]
        for dist in range(reach - 1, -1, -1):
            carried = shift_up(carried.astype(jnp.bfloat16), "seq", -1).astype(jnp.float32) + parts[dist]
        return carried
    odds = list(range(1, reach + 1, 2))
    received = swap_partner([parts[s] for s in odds], "seq")
    summed = {}
    for dist in range(0, reach + 2, 2):
        zero = jnp.zeros_like(parts[0])
        from_core1 = received[dist // 2] if dist // 2 < len(odds) else zero
        from_core0 = received[dist // 2 - 1] if dist >= 2 and dist // 2 - 1 < len(odds) else zero
        own = parts[dist] if dist <= reach else zero
        summed[dist] = own + jnp.where(core == 0, from_core1, from_core0)
    count = lax.axis_size("seq")
    if reach == 4 and count % 4 == 0:
        row = (lax.axis_index("seq") // 2) % 2
        later = [i for i in range(count) if (i // 2) % 2 == 1]
        earlier = [i for i in range(count) if (i // 2) % 2 == 0 and i + 2 < count]
        near = summed[2].astype(jnp.bfloat16)
        direct = lax.ppermute(near, "seq", [(i, i - 2) for i in later])
        relayed = lax.ppermute(near, "seq", [(i, i + 2) for i in earlier])
        far = summed[4] + jnp.where(row == 1, relayed.astype(jnp.float32), 0.0)
        total = summed[0] + jnp.where(row == 0, direct.astype(jnp.float32), 0.0)
        return total + shift_up(far.astype(jnp.bfloat16), "seq", -4).astype(jnp.float32)
    total = summed[0]
    for dist in range(2, reach + 2, 2):
        total = total + shift_up(summed[dist].astype(jnp.bfloat16), "seq", -dist).astype(jnp.float32)
    return total


def local(query_rows, key_rows, value_rows, out_grad, lengths, out_weight):
    seq_count = lax.axis_size("seq")
    device = lax.axis_index("seq")
    core = device % 2
    paired = seq_count % 2 == 0
    tok_rows = query_rows.shape[1]
    feature_width = query_rows.shape[2]
    total_frames = seq_count * tok_rows
    reach = min(-(-MOST // tok_rows), seq_count - 1)
    score_scale = HEAD_DIM ** (-0.5)
    utt_lengths = lengths[0]

    weight_cols = lax.all_gather(out_weight, "dp", axis=1, tiled=True)
    weight_full = lax.all_gather(weight_cols, "seq", axis=0, tiled=True)

    query_heads = head_major(query_rows[0], tok_rows)
    own_kv = jnp.stack([head_major(key_rows[0], tok_rows), head_major(value_rows[0], tok_rows)])
    held = gather_behind(own_kv, reach, paired, core)

    query_utt, query_stretch = frame_labels(utt_lengths, device * tok_rows, tok_rows, total_frames)
    block_visible = []
    for dist in range(reach + 1):
        key_utt, key_stretch = frame_labels(
            utt_lengths, (device - dist) * tok_rows, tok_rows, total_frames
        )
        block_visible.append(
            (query_utt[:, None] == key_utt[None, :]) & (key_stretch[None, :] <= query_stretch[:, None])
        )

    block_scores = []
    top_score = None
    for dist in range(reach + 1):
        scores = (
            jnp.einsum("hqe,hke->hqk", query_heads, held[dist][0], preferred_element_type=jnp.float32)
            * score_scale
        )
        scores = jnp.where(block_visible[dist][None], scores, MASKED_SCORE)
        block_scores.append(scores)
        block_top = jnp.max(scores, axis=2)
        top_score = block_top if top_score is None else jnp.maximum(top_score, block_top)
    row_sum = None
    weighted = None
    for dist in range(reach + 1):
        expo_full = jnp.where(
            block_visible[dist][None], jnp.exp(block_scores[dist] - top_score[:, :, None]), 0.0
        )
        part_sum = jnp.sum(expo_full, axis=2)
        product = jnp.einsum(
            "hqk,hke->hqe",
            expo_full.astype(jnp.bfloat16),
            held[dist][1],
            preferred_element_type=jnp.float32,
        )
        row_sum = part_sum if row_sum is None else row_sum + part_sum
        weighted = product if weighted is None else weighted + product
    attended_heads = (weighted / row_sum[:, :, None]).astype(jnp.bfloat16)
    attended = row_major(attended_heads, tok_rows)
    log_sum = top_score + jnp.log(row_sum)

    mixed_out = jnp.dot(attended, weight_full, preferred_element_type=jnp.float32).astype(
        jnp.bfloat16
    )
    upstream = out_grad[0]
    att_grad = lax.dot_general(
        upstream, weight_full, (((1,), (1,)), ((), ())), preferred_element_type=jnp.float32
    ).astype(jnp.bfloat16)

    partial_weight = lax.dot_general(
        attended, upstream, (((0,), (0,)), ((), ())), preferred_element_type=jnp.float32
    )
    row_share = lax.psum_scatter(
        partial_weight.astype(jnp.bfloat16), "seq", scatter_dimension=0, tiled=True
    )
    weight_grad = lax.psum_scatter(
        row_share.astype(jnp.float32), "dp", scatter_dimension=1, tiled=True
    )

    grad_heads = head_major(att_grad, tok_rows)
    delta_rows = jnp.sum(
        grad_heads.astype(jnp.float32) * attended_heads.astype(jnp.float32), axis=2
    )

    query_acc = None
    parts = [None] * (reach + 1)
    order = [d for d in range(reach, -1, -1) if d % 2 == 1] + [
        d for d in range(reach, -1, -1) if d % 2 == 0
    ]
    for dist in order:
        key_block = held[dist][0]
        value_block = held[dist][1]
        scores = (
            jnp.einsum("hqe,hke->hqk", query_heads, key_block, preferred_element_type=jnp.float32)
            * score_scale
        )
        prob_full = jnp.where(
            block_visible[dist][None], jnp.exp(scores - log_sum[:, :, None]), 0.0
        )
        prob_back = prob_full.astype(jnp.bfloat16)
        prob_grad = jnp.einsum(
            "hqe,hke->hqk", grad_heads, value_block, preferred_element_type=jnp.float32
        )
        score_grad = (prob_full * (prob_grad - delta_rows[:, :, None])).astype(jnp.bfloat16)
        query_part = jnp.einsum(
            "hqk,hke->hqe", score_grad, key_block, preferred_element_type=jnp.float32
        )
        query_acc = query_part if query_acc is None else query_acc + query_part
        key_part = (
            jnp.einsum("hqk,hqe->hke", score_grad, query_heads, preferred_element_type=jnp.float32)
            * score_scale
        )
        value_part = jnp.einsum(
            "hqk,hqe->hke", prob_back, grad_heads, preferred_element_type=jnp.float32
        )
        parts[dist] = jnp.stack([key_part, value_part])

    kv_grad = return_behind(parts, reach, paired, core)
    query_grad = row_major(query_acc * score_scale, tok_rows).astype(jnp.bfloat16)
    key_grad = row_major(kv_grad[0], tok_rows).astype(jnp.bfloat16)
    value_grad = row_major(kv_grad[1], tok_rows).astype(jnp.bfloat16)
    return (mixed_out[None], query_grad[None], key_grad[None], value_grad[None], weight_grad)


def solution(mesh):
    return jax.shard_map(
        local,
        mesh=mesh,
        in_specs=(
            P("dp", "seq", None),
            P("dp", "seq", None),
            P("dp", "seq", None),
            P("dp", "seq", None),
            P("dp", None),
            P("seq", "dp"),
        ),
        out_specs=(
            P("dp", "seq", None),
            P("dp", "seq", None),
            P("dp", "seq", None),
            P("dp", "seq", None),
            P("seq", "dp"),
        ),
        check_vma=False,
    )
```

```python
import jax
import jax.numpy as jnp
from jax import lax
from jax.sharding import PartitionSpec as P

HEADS = 12
HEAD_DIM = 64
STRETCH = 128
MOST = 1024


MASKED_SCORE = -1e30


def shift_up(block, axis, distance):
    devices = range(lax.axis_size(axis))
    route = [(i - distance, i) for i in devices if i - distance in devices]
    return lax.ppermute(block, axis, route)


def swap_partner(block, axis):
    count = lax.axis_size(axis)
    return lax.ppermute(block, axis, [(i, i ^ 1) for i in range(count)])


def frame_labels(utt_lengths, first_frame, frame_count, total_frames):
    positions = first_frame + jnp.arange(frame_count, dtype=jnp.int32)
    utt_ends = jnp.cumsum(utt_lengths)
    utt_index = jnp.sum((positions[:, None] >= utt_ends[None, :]).astype(jnp.int32), axis=1)
    outside = (positions < 0) | (positions >= total_frames)
    return (jnp.where(outside, -1, utt_index), positions // STRETCH)


def head_major(rows, tok_rows):
    return jnp.transpose(rows.reshape(tok_rows, HEADS, HEAD_DIM), (1, 0, 2))


def row_major(heads, tok_rows):
    return jnp.transpose(heads, (1, 0, 2)).reshape(tok_rows, HEADS * HEAD_DIM)


def gather_behind(own, reach, paired, core):
    if not paired:
        held = [own]
        for _ in range(reach):
            held.append(shift_up(held[-1], "seq", 1))
        return held
    evens = {0: own}
    count = lax.axis_size("seq")
    if reach == 4 and count % 4 == 0:
        row = (lax.axis_index("seq") // 2) % 2
        later = [i for i in range(count) if (i // 2) % 2 == 1]
        earlier = [i for i in range(count) if (i // 2) % 2 == 0 and i + 2 < count]
        far = [shift_up(own[k], "seq", 4) for k in range(2)]
        near = []
        for k in range(2):
            direct = lax.ppermute(own[k], "seq", [(i - 2, i) for i in later])
            relayed = lax.ppermute(far[k], "seq", [(i + 2, i) for i in earlier])
            near.append(jnp.where(row == 1, direct, relayed))
        evens[2] = jnp.stack(near)
        evens[4] = jnp.stack(far)
    else:
        for dist in range(2, reach + 2, 2):
            evens[dist] = shift_up(own, "seq", dist)
    odds = list(range(1, reach + 1, 2))
    payload = [jnp.where(core == 0, evens[s - 1], evens[s + 1]) for s in odds]
    received = swap_partner(payload, "seq")
    held = []
    for dist in range(reach + 1):
        held.append(evens[dist] if dist % 2 == 0 else received[(dist - 1) // 2])
    return held


def return_behind(parts, reach, paired, core):
    if not paired:
        carried = parts[reach]
        for dist in range(reach - 1, -1, -1):
            carried = shift_up(carried.astype(jnp.bfloat16), "seq", -1).astype(jnp.float32) + parts[dist]
        return carried
    odds = list(range(1, reach + 1, 2))
    received = swap_partner([parts[s] for s in odds], "seq")
    summed = {}
    for dist in range(0, reach + 2, 2):
        zero = jnp.zeros_like(parts[0])
        from_core1 = received[dist // 2] if dist // 2 < len(odds) else zero
        from_core0 = received[dist // 2 - 1] if dist >= 2 and dist // 2 - 1 < len(odds) else zero
        own = parts[dist] if dist <= reach else zero
        summed[dist] = own + jnp.where(core == 0, from_core1, from_core0)
    count = lax.axis_size("seq")
    if reach == 4 and count % 4 == 0:
        row = (lax.axis_index("seq") // 2) % 2
        later = [i for i in range(count) if (i // 2) % 2 == 1]
        earlier = [i for i in range(count) if (i // 2) % 2 == 0 and i + 2 < count]
        near = summed[2].astype(jnp.bfloat16)
        direct = lax.ppermute(near, "seq", [(i, i - 2) for i in later])
        relayed = lax.ppermute(near, "seq", [(i, i + 2) for i in earlier])
        far = summed[4] + jnp.where(row == 1, relayed.astype(jnp.float32), 0.0)
        total = summed[0] + jnp.where(row == 0, direct.astype(jnp.float32), 0.0)
        return total + shift_up(far.astype(jnp.bfloat16), "seq", -4).astype(jnp.float32)
    total = summed[0]
    for dist in range(2, reach + 2, 2):
        total = total + shift_up(summed[dist].astype(jnp.bfloat16), "seq", -dist).astype(jnp.float32)
    return total


def local(query_rows, key_rows, value_rows, out_grad, lengths, out_weight):
    seq_count = lax.axis_size("seq")
    device = lax.axis_index("seq")
    core = device % 2
    paired = seq_count % 2 == 0
    tok_rows = query_rows.shape[1]
    feature_width = query_rows.shape[2]
    total_frames = seq_count * tok_rows
    reach = min(-(-MOST // tok_rows), seq_count - 1)
    score_scale = HEAD_DIM ** (-0.5)
    utt_lengths = lengths[0]

    weight_rows = lax.all_gather(out_weight, "seq", axis=0, tiled=True)
    weight_full = lax.all_gather(weight_rows, "dp", axis=1, tiled=True)

    query_heads = head_major(query_rows[0], tok_rows)
    own_kv = jnp.stack([head_major(key_rows[0], tok_rows), head_major(value_rows[0], tok_rows)])
    held = gather_behind(own_kv, reach, paired, core)

    query_utt, query_stretch = frame_labels(utt_lengths, device * tok_rows, tok_rows, total_frames)
    block_visible = []
    for dist in range(reach + 1):
        key_utt, key_stretch = frame_labels(
            utt_lengths, (device - dist) * tok_rows, tok_rows, total_frames
        )
        block_visible.append(
            (query_utt[:, None] == key_utt[None, :]) & (key_stretch[None, :] <= query_stretch[:, None])
        )

    block_scores = []
    top_score = None
    for dist in range(reach + 1):
        scores = (
            jnp.einsum("hqe,hke->hqk", query_heads, held[dist][0], preferred_element_type=jnp.float32)
            * score_scale
        )
        scores = jnp.where(block_visible[dist][None], scores, MASKED_SCORE)
        block_scores.append(scores)
        block_top = jnp.max(scores, axis=2)
        top_score = block_top if top_score is None else jnp.maximum(top_score, block_top)
    row_sum = None
    weighted = None
    for dist in range(reach + 1):
        expo_full = jnp.where(
            block_visible[dist][None], jnp.exp(block_scores[dist] - top_score[:, :, None]), 0.0
        )
        part_sum = jnp.sum(expo_full, axis=2)
        product = jnp.einsum(
            "hqk,hke->hqe",
            expo_full.astype(jnp.bfloat16),
            held[dist][1],
            preferred_element_type=jnp.float32,
        )
        row_sum = part_sum if row_sum is None else row_sum + part_sum
        weighted = product if weighted is None else weighted + product
    attended_heads = (weighted / row_sum[:, :, None]).astype(jnp.bfloat16)
    attended = row_major(attended_heads, tok_rows)
    log_sum = top_score + jnp.log(row_sum)

    mixed_out = jnp.dot(attended, weight_full, preferred_element_type=jnp.float32).astype(
        jnp.bfloat16
    )
    upstream = out_grad[0]
    att_grad = lax.dot_general(
        upstream, weight_full, (((1,), (1,)), ((), ())), preferred_element_type=jnp.float32
    ).astype(jnp.bfloat16)

    partial_weight = lax.dot_general(
        attended, upstream, (((0,), (0,)), ((), ())), preferred_element_type=jnp.float32
    )
    row_share = lax.psum_scatter(
        partial_weight.astype(jnp.bfloat16), "seq", scatter_dimension=0, tiled=True
    )
    weight_grad = lax.psum_scatter(
        row_share.astype(jnp.float32), "dp", scatter_dimension=1, tiled=True
    )

    grad_heads = head_major(att_grad, tok_rows)
    delta_rows = jnp.sum(
        grad_heads.astype(jnp.float32) * attended_heads.astype(jnp.float32), axis=2
    )

    query_acc = None
    parts = [None] * (reach + 1)
    order = [d for d in range(reach, -1, -1) if d % 2 == 1] + [
        d for d in range(reach, -1, -1) if d % 2 == 0
    ]
    for dist in order:
        key_block = held[dist][0]
        value_block = held[dist][1]
        scores = (
            jnp.einsum("hqe,hke->hqk", query_heads, key_block, preferred_element_type=jnp.float32)
            * score_scale
        )
        prob_full = jnp.where(
            block_visible[dist][None], jnp.exp(scores - log_sum[:, :, None]), 0.0
        )
        prob_back = prob_full.astype(jnp.bfloat16)
        prob_grad = jnp.einsum(
            "hqe,hke->hqk", grad_heads, value_block, preferred_element_type=jnp.float32
        )
        score_grad = (prob_full * (prob_grad - delta_rows[:, :, None])).astype(jnp.bfloat16)
        query_part = jnp.einsum(
            "hqk,hke->hqe", score_grad, key_block, preferred_element_type=jnp.float32
        )
        query_acc = query_part if query_acc is None else query_acc + query_part
        key_part = (
            jnp.einsum("hqk,hqe->hke", score_grad, query_heads, preferred_element_type=jnp.float32)
            * score_scale
        )
        value_part = jnp.einsum(
            "hqk,hqe->hke", prob_back, grad_heads, preferred_element_type=jnp.float32
        )
        parts[dist] = jnp.stack([key_part, value_part])

    kv_grad = return_behind(parts, reach, paired, core)
    query_grad = row_major(query_acc * score_scale, tok_rows).astype(jnp.bfloat16)
    key_grad = row_major(kv_grad[0], tok_rows).astype(jnp.bfloat16)
    value_grad = row_major(kv_grad[1], tok_rows).astype(jnp.bfloat16)
    return (mixed_out[None], query_grad[None], key_grad[None], value_grad[None], weight_grad)


def solution(mesh):
    return jax.shard_map(
        local,
        mesh=mesh,
        in_specs=(
            P("dp", "seq", None),
            P("dp", "seq", None),
            P("dp", "seq", None),
            P("dp", "seq", None),
            P("dp", None),
            P("seq", "dp"),
        ),
        out_specs=(
            P("dp", "seq", None),
            P("dp", "seq", None),
            P("dp", "seq", None),
            P("dp", "seq", None),
            P("seq", "dp"),
        ),
        check_vma=False,
    )
```

```python
import jax
import jax.numpy as jnp
from jax import lax
from jax.sharding import PartitionSpec as P

HEADS = 12
HEAD_DIM = 64
STRETCH = 128
MOST = 1024


MASKED_SCORE = -1e30


def shift_up(block, axis, distance):
    devices = range(lax.axis_size(axis))
    route = [(i - distance, i) for i in devices if i - distance in devices]
    return lax.ppermute(block, axis, route)


def swap_partner(block, axis):
    count = lax.axis_size(axis)
    return lax.ppermute(block, axis, [(i, i ^ 1) for i in range(count)])


def halving_scatter(total, axis, dim, sends_narrow):
    count = lax.axis_size(axis)
    if count & (count - 1):
        return lax.psum_scatter(total, axis, scatter_dimension=dim, tiled=True)
    me = lax.axis_index(axis)
    bits = count.bit_length() - 1
    moved = jnp.moveaxis(total, dim, 0)
    rest = moved.shape[1:]
    blocks = moved.reshape((2,) * bits + (moved.shape[0] // count,) + rest)
    for step in range(bits):
        own_bit = (me >> step) % 2
        keep = lax.dynamic_index_in_dim(blocks, own_bit, blocks.ndim - len(rest) - 2, keepdims=False)
        give = lax.dynamic_index_in_dim(blocks, 1 - own_bit, blocks.ndim - len(rest) - 2, keepdims=False)
        if sends_narrow[step]:
            give = give.astype(jnp.bfloat16)
        got = lax.ppermute(give, axis, [(i, i ^ (1 << step)) for i in range(count)])
        blocks = keep + got.astype(keep.dtype)
    return jnp.moveaxis(blocks, 0, dim)


def frame_labels(utt_lengths, first_frame, frame_count, total_frames):
    positions = first_frame + jnp.arange(frame_count, dtype=jnp.int32)
    utt_ends = jnp.cumsum(utt_lengths)
    utt_index = jnp.sum((positions[:, None] >= utt_ends[None, :]).astype(jnp.int32), axis=1)
    outside = (positions < 0) | (positions >= total_frames)
    return (jnp.where(outside, -1, utt_index), positions // STRETCH)


def head_major(rows, tok_rows):
    return jnp.transpose(rows.reshape(tok_rows, HEADS, HEAD_DIM), (1, 0, 2))


def row_major(heads, tok_rows):
    return jnp.transpose(heads, (1, 0, 2)).reshape(tok_rows, HEADS * HEAD_DIM)


def gather_behind(own, reach, paired, core):
    if not paired:
        held = [own]
        for _ in range(reach):
            held.append(shift_up(held[-1], "seq", 1))
        return held
    evens = {0: own}
    count = lax.axis_size("seq")
    if reach == 4 and count % 4 == 0:
        row = (lax.axis_index("seq") // 2) % 2
        later = [i for i in range(count) if (i // 2) % 2 == 1]
        earlier = [i for i in range(count) if (i // 2) % 2 == 0 and i + 2 < count]
        far = [shift_up(own[k], "seq", 4) for k in range(2)]
        near = []
        for k in range(2):
            direct = lax.ppermute(own[k], "seq", [(i - 2, i) for i in later])
            relayed = lax.ppermute(far[k], "seq", [(i + 2, i) for i in earlier])
            near.append(jnp.where(row == 1, direct, relayed))
        evens[2] = jnp.stack(near)
        evens[4] = jnp.stack(far)
    else:
        for dist in range(2, reach + 2, 2):
            evens[dist] = shift_up(own, "seq", dist)
    odds = list(range(1, reach + 1, 2))
    payload = [jnp.where(core == 0, evens[s - 1], evens[s + 1]) for s in odds]
    received = swap_partner(payload, "seq")
    held = []
    for dist in range(reach + 1):
        held.append(evens[dist] if dist % 2 == 0 else received[(dist - 1) // 2])
    return held


def return_behind(parts, reach, paired, core):
    if not paired:
        carried = parts[reach]
        for dist in range(reach - 1, -1, -1):
            carried = shift_up(carried.astype(jnp.bfloat16), "seq", -1).astype(jnp.float32) + parts[dist]
        return carried
    odds = list(range(1, reach + 1, 2))
    received = swap_partner([parts[s] for s in odds], "seq")
    summed = {}
    for dist in range(0, reach + 2, 2):
        zero = jnp.zeros_like(parts[0])
        from_core1 = received[dist // 2] if dist // 2 < len(odds) else zero
        from_core0 = received[dist // 2 - 1] if dist >= 2 and dist // 2 - 1 < len(odds) else zero
        own = parts[dist] if dist <= reach else zero
        summed[dist] = own + jnp.where(core == 0, from_core1, from_core0)
    count = lax.axis_size("seq")
    if reach == 4 and count % 4 == 0:
        row = (lax.axis_index("seq") // 2) % 2
        later = [i for i in range(count) if (i // 2) % 2 == 1]
        earlier = [i for i in range(count) if (i // 2) % 2 == 0 and i + 2 < count]
        near = summed[2].astype(jnp.bfloat16)
        direct = lax.ppermute(near, "seq", [(i, i - 2) for i in later])
        relayed = lax.ppermute(near, "seq", [(i, i + 2) for i in earlier])
        far = summed[4] + jnp.where(row == 1, relayed.astype(jnp.float32), 0.0)
        total = summed[0] + jnp.where(row == 0, direct.astype(jnp.float32), 0.0)
        return total + shift_up(far.astype(jnp.bfloat16), "seq", -4).astype(jnp.float32)
    total = summed[0]
    for dist in range(2, reach + 2, 2):
        total = total + shift_up(summed[dist].astype(jnp.bfloat16), "seq", -dist).astype(jnp.float32)
    return total


def local(query_rows, key_rows, value_rows, out_grad, lengths, out_weight):
    seq_count = lax.axis_size("seq")
    device = lax.axis_index("seq")
    core = device % 2
    paired = seq_count % 2 == 0
    tok_rows = query_rows.shape[1]
    feature_width = query_rows.shape[2]
    total_frames = seq_count * tok_rows
    reach = min(-(-MOST // tok_rows), seq_count - 1)
    score_scale = HEAD_DIM ** (-0.5)
    utt_lengths = lengths[0]

    weight_cols = lax.all_gather(out_weight, "dp", axis=1, tiled=True)
    weight_full = lax.all_gather(weight_cols, "seq", axis=0, tiled=True)

    query_heads = head_major(query_rows[0], tok_rows)
    own_kv = jnp.stack([head_major(key_rows[0], tok_rows), head_major(value_rows[0], tok_rows)])
    held = gather_behind(own_kv, reach, paired, core)

    query_utt, query_stretch = frame_labels(utt_lengths, device * tok_rows, tok_rows, total_frames)
    block_visible = []
    for dist in range(reach + 1):
        key_utt, key_stretch = frame_labels(
            utt_lengths, (device - dist) * tok_rows, tok_rows, total_frames
        )
        block_visible.append(
            (query_utt[:, None] == key_utt[None, :]) & (key_stretch[None, :] <= query_stretch[:, None])
        )

    block_scores = []
    top_score = None
    for dist in range(reach + 1):
        scores = (
            jnp.einsum("hqe,hke->hqk", query_heads, held[dist][0], preferred_element_type=jnp.float32)
            * score_scale
        )
        scores = jnp.where(block_visible[dist][None], scores, MASKED_SCORE)
        block_scores.append(scores)
        block_top = jnp.max(scores, axis=2)
        top_score = block_top if top_score is None else jnp.maximum(top_score, block_top)
    row_sum = None
    weighted = None
    for dist in range(reach + 1):
        expo_full = jnp.where(
            block_visible[dist][None], jnp.exp(block_scores[dist] - top_score[:, :, None]), 0.0
        )
        part_sum = jnp.sum(expo_full, axis=2)
        product = jnp.einsum(
            "hqk,hke->hqe",
            expo_full.astype(jnp.bfloat16),
            held[dist][1],
            preferred_element_type=jnp.float32,
        )
        row_sum = part_sum if row_sum is None else row_sum + part_sum
        weighted = product if weighted is None else weighted + product
    attended_heads = (weighted / row_sum[:, :, None]).astype(jnp.bfloat16)
    attended = row_major(attended_heads, tok_rows)
    log_sum = top_score + jnp.log(row_sum)

    mixed_out = jnp.dot(attended, weight_full, preferred_element_type=jnp.float32).astype(
        jnp.bfloat16
    )
    upstream = out_grad[0]
    att_grad = lax.dot_general(
        upstream, weight_full, (((1,), (1,)), ((), ())), preferred_element_type=jnp.float32
    ).astype(jnp.bfloat16)

    partial_weight = lax.dot_general(
        attended, upstream, (((0,), (0,)), ((), ())), preferred_element_type=jnp.float32
    )
    row_share = lax.psum_scatter(
        partial_weight.astype(jnp.bfloat16), "seq", scatter_dimension=0, tiled=True
    )
    weight_grad = halving_scatter(row_share.astype(jnp.float32), "dp", 1, [False] * 8)

    grad_heads = head_major(att_grad, tok_rows)
    delta_rows = jnp.sum(
        grad_heads.astype(jnp.float32) * attended_heads.astype(jnp.float32), axis=2
    )

    query_acc = None
    parts = [None] * (reach + 1)
    order = [d for d in range(reach, -1, -1) if d % 2 == 1] + [
        d for d in range(reach, -1, -1) if d % 2 == 0
    ]
    for dist in order:
        key_block = held[dist][0]
        value_block = held[dist][1]
        scores = (
            jnp.einsum("hqe,hke->hqk", query_heads, key_block, preferred_element_type=jnp.float32)
            * score_scale
        )
        prob_full = jnp.where(
            block_visible[dist][None], jnp.exp(scores - log_sum[:, :, None]), 0.0
        )
        prob_back = prob_full.astype(jnp.bfloat16)
        prob_grad = jnp.einsum(
            "hqe,hke->hqk", grad_heads, value_block, preferred_element_type=jnp.float32
        )
        score_grad = (prob_full * (prob_grad - delta_rows[:, :, None])).astype(jnp.bfloat16)
        query_part = jnp.einsum(
            "hqk,hke->hqe", score_grad, key_block, preferred_element_type=jnp.float32
        )
        query_acc = query_part if query_acc is None else query_acc + query_part
        key_part = (
            jnp.einsum("hqk,hqe->hke", score_grad, query_heads, preferred_element_type=jnp.float32)
            * score_scale
        )
        value_part = jnp.einsum(
            "hqk,hqe->hke", prob_back, grad_heads, preferred_element_type=jnp.float32
        )
        parts[dist] = jnp.stack([key_part, value_part])

    kv_grad = return_behind(parts, reach, paired, core)
    query_grad = row_major(query_acc * score_scale, tok_rows).astype(jnp.bfloat16)
    key_grad = row_major(kv_grad[0], tok_rows).astype(jnp.bfloat16)
    value_grad = row_major(kv_grad[1], tok_rows).astype(jnp.bfloat16)
    return (mixed_out[None], query_grad[None], key_grad[None], value_grad[None], weight_grad)


def solution(mesh):
    return jax.shard_map(
        local,
        mesh=mesh,
        in_specs=(
            P("dp", "seq", None),
            P("dp", "seq", None),
            P("dp", "seq", None),
            P("dp", "seq", None),
            P("dp", None),
            P("seq", "dp"),
        ),
        out_specs=(
            P("dp", "seq", None),
            P("dp", "seq", None),
            P("dp", "seq", None),
            P("dp", "seq", None),
            P("seq", "dp"),
        ),
        check_vma=False,
    )
```

```python
import jax
import jax.numpy as jnp
from jax import lax
from jax.sharding import PartitionSpec as P

HEADS = 12
HEAD_DIM = 64
STRETCH = 128
MOST = 1024


MASKED_SCORE = -1e30


def shift_up(block, axis, distance):
    devices = range(lax.axis_size(axis))
    route = [(i - distance, i) for i in devices if i - distance in devices]
    return lax.ppermute(block, axis, route)


def swap_partner(block, axis):
    count = lax.axis_size(axis)
    return lax.ppermute(block, axis, [(i, i ^ 1) for i in range(count)])


def frame_labels(utt_lengths, first_frame, frame_count, total_frames):
    positions = first_frame + jnp.arange(frame_count, dtype=jnp.int32)
    utt_ends = jnp.cumsum(utt_lengths)
    utt_index = jnp.sum((positions[:, None] >= utt_ends[None, :]).astype(jnp.int32), axis=1)
    outside = (positions < 0) | (positions >= total_frames)
    return (jnp.where(outside, -1, utt_index), positions // STRETCH)


def head_major(rows, tok_rows):
    return jnp.transpose(rows.reshape(tok_rows, HEADS, HEAD_DIM), (1, 0, 2))


def row_major(heads, tok_rows):
    return jnp.transpose(heads, (1, 0, 2)).reshape(tok_rows, HEADS * HEAD_DIM)


def gather_behind(own, reach, paired, core):
    if not paired:
        held = [own]
        for _ in range(reach):
            held.append(shift_up(held[-1], "seq", 1))
        return held
    evens = {0: own}
    count = lax.axis_size("seq")
    if reach == 4 and count % 4 == 0:
        row = (lax.axis_index("seq") // 2) % 2
        later = [i for i in range(count) if (i // 2) % 2 == 1]
        earlier = [i for i in range(count) if (i // 2) % 2 == 0 and i + 2 < count]
        far = [shift_up(own[k], "seq", 4) for k in range(2)]
        near = []
        for k in range(2):
            direct = lax.ppermute(own[k], "seq", [(i - 2, i) for i in later])
            relayed = lax.ppermute(far[k], "seq", [(i + 2, i) for i in earlier])
            near.append(jnp.where(row == 1, direct, relayed))
        evens[2] = jnp.stack(near)
        evens[4] = jnp.stack(far)
    else:
        for dist in range(2, reach + 2, 2):
            evens[dist] = shift_up(own, "seq", dist)
    odds = list(range(1, reach + 1, 2))
    payload = [jnp.where(core == 0, evens[s - 1], evens[s + 1]) for s in odds]
    received = swap_partner(payload, "seq")
    held = []
    for dist in range(reach + 1):
        held.append(evens[dist] if dist % 2 == 0 else received[(dist - 1) // 2])
    return held


def return_behind(parts, reach, paired, core):
    if not paired:
        carried = parts[reach]
        for dist in range(reach - 1, -1, -1):
            carried = shift_up(carried.astype(jnp.bfloat16), "seq", -1).astype(jnp.float32) + parts[dist]
        return carried
    odds = list(range(1, reach + 1, 2))
    received = swap_partner([parts[s] for s in odds], "seq")
    summed = {}
    for dist in range(0, reach + 2, 2):
        zero = jnp.zeros_like(parts[0])
        from_core1 = received[dist // 2] if dist // 2 < len(odds) else zero
        from_core0 = received[dist // 2 - 1] if dist >= 2 and dist // 2 - 1 < len(odds) else zero
        own = parts[dist] if dist <= reach else zero
        summed[dist] = own + jnp.where(core == 0, from_core1, from_core0)
    count = lax.axis_size("seq")
    if reach == 4 and count % 4 == 0:
        row = (lax.axis_index("seq") // 2) % 2
        later = [i for i in range(count) if (i // 2) % 2 == 1]
        earlier = [i for i in range(count) if (i // 2) % 2 == 0 and i + 2 < count]
        near = summed[2].astype(jnp.bfloat16)
        direct = lax.ppermute(near, "seq", [(i, i - 2) for i in later])
        relayed = lax.ppermute(near, "seq", [(i, i + 2) for i in earlier])
        far = summed[4] + jnp.where(row == 1, relayed.astype(jnp.float32), 0.0)
        total = summed[0] + jnp.where(row == 0, direct.astype(jnp.float32), 0.0)
        return total + shift_up(far.astype(jnp.bfloat16), "seq", -4).astype(jnp.float32)
    total = summed[0]
    for dist in range(2, reach + 2, 2):
        total = total + shift_up(summed[dist].astype(jnp.bfloat16), "seq", -dist).astype(jnp.float32)
    return total


def local(query_rows, key_rows, value_rows, out_grad, lengths, out_weight):
    seq_count = lax.axis_size("seq")
    device = lax.axis_index("seq")
    core = device % 2
    paired = seq_count % 2 == 0
    tok_rows = query_rows.shape[1]
    feature_width = query_rows.shape[2]
    total_frames = seq_count * tok_rows
    reach = min(-(-MOST // tok_rows), seq_count - 1)
    score_scale = HEAD_DIM ** (-0.5)
    utt_lengths = lengths[0]

    row_blocks, col_blocks = lax.axis_size("seq"), lax.axis_size("dp")
    pieces = lax.all_gather(out_weight, ("seq", "dp"), axis=0, tiled=False)
    weight_full = jnp.transpose(
        pieces.reshape((row_blocks, col_blocks) + out_weight.shape), (0, 2, 1, 3)
    ).reshape(row_blocks * out_weight.shape[0], col_blocks * out_weight.shape[1])

    query_heads = head_major(query_rows[0], tok_rows)
    own_kv = jnp.stack([head_major(key_rows[0], tok_rows), head_major(value_rows[0], tok_rows)])
    held = gather_behind(own_kv, reach, paired, core)

    query_utt, query_stretch = frame_labels(utt_lengths, device * tok_rows, tok_rows, total_frames)
    block_visible = []
    for dist in range(reach + 1):
        key_utt, key_stretch = frame_labels(
            utt_lengths, (device - dist) * tok_rows, tok_rows, total_frames
        )
        block_visible.append(
            (query_utt[:, None] == key_utt[None, :]) & (key_stretch[None, :] <= query_stretch[:, None])
        )

    block_scores = []
    top_score = None
    for dist in range(reach + 1):
        scores = (
            jnp.einsum("hqe,hke->hqk", query_heads, held[dist][0], preferred_element_type=jnp.float32)
            * score_scale
        )
        scores = jnp.where(block_visible[dist][None], scores, MASKED_SCORE)
        block_scores.append(scores)
        block_top = jnp.max(scores, axis=2)
        top_score = block_top if top_score is None else jnp.maximum(top_score, block_top)
    row_sum = None
    weighted = None
    for dist in range(reach + 1):
        expo_full = jnp.where(
            block_visible[dist][None], jnp.exp(block_scores[dist] - top_score[:, :, None]), 0.0
        )
        part_sum = jnp.sum(expo_full, axis=2)
        product = jnp.einsum(
            "hqk,hke->hqe",
            expo_full.astype(jnp.bfloat16),
            held[dist][1],
            preferred_element_type=jnp.float32,
        )
        row_sum = part_sum if row_sum is None else row_sum + part_sum
        weighted = product if weighted is None else weighted + product
    attended_heads = (weighted / row_sum[:, :, None]).astype(jnp.bfloat16)
    attended = row_major(attended_heads, tok_rows)
    log_sum = top_score + jnp.log(row_sum)

    upstream = out_grad[0]
    partial_weight = lax.dot_general(
        attended, upstream, (((0,), (0,)), ((), ())), preferred_element_type=jnp.float32
    )
    partial_weight, attended = lax.optimization_barrier((partial_weight, attended))
    mixed_out = jnp.dot(attended, weight_full, preferred_element_type=jnp.float32).astype(
        jnp.bfloat16
    )
    att_grad = lax.dot_general(
        upstream, weight_full, (((1,), (1,)), ((), ())), preferred_element_type=jnp.float32
    ).astype(jnp.bfloat16)

    row_share = lax.psum_scatter(
        partial_weight.astype(jnp.bfloat16), "seq", scatter_dimension=0, tiled=True
    )
    weight_grad = lax.psum_scatter(
        row_share.astype(jnp.float32), "dp", scatter_dimension=1, tiled=True
    )

    grad_heads = head_major(att_grad, tok_rows)
    delta_rows = jnp.sum(
        grad_heads.astype(jnp.float32) * attended_heads.astype(jnp.float32), axis=2
    )

    query_acc = None
    parts = [None] * (reach + 1)
    order = [d for d in range(reach, -1, -1) if d % 2 == 1] + [
        d for d in range(reach, -1, -1) if d % 2 == 0
    ]
    for dist in order:
        key_block = held[dist][0]
        value_block = held[dist][1]
        scores = (
            jnp.einsum("hqe,hke->hqk", query_heads, key_block, preferred_element_type=jnp.float32)
            * score_scale
        )
        prob_full = jnp.where(
            block_visible[dist][None], jnp.exp(scores - log_sum[:, :, None]), 0.0
        )
        prob_back = prob_full.astype(jnp.bfloat16)
        prob_grad = jnp.einsum(
            "hqe,hke->hqk", grad_heads, value_block, preferred_element_type=jnp.float32
        )
        score_grad = (prob_full * (prob_grad - delta_rows[:, :, None])).astype(jnp.bfloat16)
        query_part = jnp.einsum(
            "hqk,hke->hqe", score_grad, key_block, preferred_element_type=jnp.float32
        )
        query_acc = query_part if query_acc is None else query_acc + query_part
        key_part = (
            jnp.einsum("hqk,hqe->hke", score_grad, query_heads, preferred_element_type=jnp.float32)
            * score_scale
        )
        value_part = jnp.einsum(
            "hqk,hqe->hke", prob_back, grad_heads, preferred_element_type=jnp.float32
        )
        parts[dist] = jnp.stack([key_part, value_part])

    kv_grad = return_behind(parts, reach, paired, core)
    query_grad = row_major(query_acc * score_scale, tok_rows).astype(jnp.bfloat16)
    key_grad = row_major(kv_grad[0], tok_rows).astype(jnp.bfloat16)
    value_grad = row_major(kv_grad[1], tok_rows).astype(jnp.bfloat16)
    return (mixed_out[None], query_grad[None], key_grad[None], value_grad[None], weight_grad)


def solution(mesh):
    return jax.shard_map(
        local,
        mesh=mesh,
        in_specs=(
            P("dp", "seq", None),
            P("dp", "seq", None),
            P("dp", "seq", None),
            P("dp", "seq", None),
            P("dp", None),
            P("seq", "dp"),
        ),
        out_specs=(
            P("dp", "seq", None),
            P("dp", "seq", None),
            P("dp", "seq", None),
            P("dp", "seq", None),
            P("seq", "dp"),
        ),
        check_vma=False,
    )
```

```python
import jax
import jax.numpy as jnp
from jax import lax
from jax.sharding import PartitionSpec as P

HEADS = 12
HEAD_DIM = 64
STRETCH = 128
MOST = 1024


MASKED_SCORE = -1e30


def shift_up(block, axis, distance):
    devices = range(lax.axis_size(axis))
    route = [(i - distance, i) for i in devices if i - distance in devices]
    return lax.ppermute(block, axis, route)


def swap_partner(block, axis):
    count = lax.axis_size(axis)
    return lax.ppermute(block, axis, [(i, i ^ 1) for i in range(count)])


def frame_labels(utt_lengths, first_frame, frame_count, total_frames):
    positions = first_frame + jnp.arange(frame_count, dtype=jnp.int32)
    utt_ends = jnp.cumsum(utt_lengths)
    utt_index = jnp.sum((positions[:, None] >= utt_ends[None, :]).astype(jnp.int32), axis=1)
    outside = (positions < 0) | (positions >= total_frames)
    return (jnp.where(outside, -1, utt_index), positions // STRETCH)


def head_major(rows, tok_rows):
    return jnp.transpose(rows.reshape(tok_rows, HEADS, HEAD_DIM), (1, 0, 2))


def row_major(heads, tok_rows):
    return jnp.transpose(heads, (1, 0, 2)).reshape(tok_rows, HEADS * HEAD_DIM)


def gather_behind(own, reach, paired, core):
    if not paired:
        held = [own]
        for _ in range(reach):
            held.append(shift_up(held[-1], "seq", 1))
        return held
    evens = {0: own}
    count = lax.axis_size("seq")
    if reach == 4 and count % 4 == 0:
        row = (lax.axis_index("seq") // 2) % 2
        later = [i for i in range(count) if (i // 2) % 2 == 1]
        earlier = [i for i in range(count) if (i // 2) % 2 == 0 and i + 2 < count]
        far = [shift_up(own[k], "seq", 4) for k in range(2)]
        near = []
        for k in range(2):
            direct = lax.ppermute(own[k], "seq", [(i - 2, i) for i in later])
            relayed = lax.ppermute(far[k], "seq", [(i + 2, i) for i in earlier])
            near.append(jnp.where(row == 1, direct, relayed))
        evens[2] = jnp.stack(near)
        evens[4] = jnp.stack(far)
    else:
        for dist in range(2, reach + 2, 2):
            evens[dist] = shift_up(own, "seq", dist)
    odds = list(range(1, reach + 1, 2))
    payload = [jnp.where(core == 0, evens[s - 1], evens[s + 1]) for s in odds]
    received = swap_partner(payload, "seq")
    held = []
    for dist in range(reach + 1):
        held.append(evens[dist] if dist % 2 == 0 else received[(dist - 1) // 2])
    return held


def return_behind(parts, reach, paired, core):
    if not paired:
        carried = parts[reach]
        for dist in range(reach - 1, -1, -1):
            carried = shift_up(carried.astype(jnp.bfloat16), "seq", -1).astype(jnp.float32) + parts[dist]
        return carried
    odds = list(range(1, reach + 1, 2))
    received = swap_partner([parts[s] for s in odds], "seq")
    summed = {}
    for dist in range(0, reach + 2, 2):
        zero = jnp.zeros_like(parts[0])
        from_core1 = received[dist // 2] if dist // 2 < len(odds) else zero
        from_core0 = received[dist // 2 - 1] if dist >= 2 and dist // 2 - 1 < len(odds) else zero
        own = parts[dist] if dist <= reach else zero
        summed[dist] = own + jnp.where(core == 0, from_core1, from_core0)
    count = lax.axis_size("seq")
    if reach == 4 and count % 4 == 0:
        row = (lax.axis_index("seq") // 2) % 2
        later = [i for i in range(count) if (i // 2) % 2 == 1]
        earlier = [i for i in range(count) if (i // 2) % 2 == 0 and i + 2 < count]
        near = summed[2].astype(jnp.bfloat16)
        direct = lax.ppermute(near, "seq", [(i, i - 2) for i in later])
        relayed = lax.ppermute(near, "seq", [(i, i + 2) for i in earlier])
        far = summed[4] + jnp.where(row == 1, relayed.astype(jnp.float32), 0.0)
        total = summed[0] + jnp.where(row == 0, direct.astype(jnp.float32), 0.0)
        return total + shift_up(far.astype(jnp.bfloat16), "seq", -4).astype(jnp.float32)
    total = summed[0]
    for dist in range(2, reach + 2, 2):
        total = total + shift_up(summed[dist].astype(jnp.bfloat16), "seq", -dist).astype(jnp.float32)
    return total


def local(query_rows, key_rows, value_rows, out_grad, lengths, out_weight):
    seq_count = lax.axis_size("seq")
    device = lax.axis_index("seq")
    core = device % 2
    paired = seq_count % 2 == 0
    tok_rows = query_rows.shape[1]
    feature_width = query_rows.shape[2]
    total_frames = seq_count * tok_rows
    reach = min(-(-MOST // tok_rows), seq_count - 1)
    score_scale = HEAD_DIM ** (-0.5)
    utt_lengths = lengths[0]

    row_blocks, col_blocks = lax.axis_size("seq"), lax.axis_size("dp")
    pieces = lax.all_gather(out_weight, ("seq", "dp"), axis=0, tiled=False)
    weight_full = jnp.transpose(
        pieces.reshape((row_blocks, col_blocks) + out_weight.shape), (0, 2, 1, 3)
    ).reshape(row_blocks * out_weight.shape[0], col_blocks * out_weight.shape[1])

    query_heads = head_major(query_rows[0], tok_rows)
    own_kv = jnp.stack([head_major(key_rows[0], tok_rows), head_major(value_rows[0], tok_rows)])
    held = gather_behind(own_kv, reach, paired, core)

    query_utt, query_stretch = frame_labels(utt_lengths, device * tok_rows, tok_rows, total_frames)
    block_visible = []
    for dist in range(reach + 1):
        key_utt, key_stretch = frame_labels(
            utt_lengths, (device - dist) * tok_rows, tok_rows, total_frames
        )
        block_visible.append(
            (query_utt[:, None] == key_utt[None, :]) & (key_stretch[None, :] <= query_stretch[:, None])
        )

    block_scores = []
    top_score = None
    for dist in range(reach + 1):
        scores = (
            jnp.einsum("hqe,hke->hqk", query_heads, held[dist][0], preferred_element_type=jnp.float32)
            * score_scale
        )
        scores = jnp.where(block_visible[dist][None], scores, MASKED_SCORE)
        block_scores.append(scores)
        block_top = jnp.max(scores, axis=2)
        top_score = block_top if top_score is None else jnp.maximum(top_score, block_top)
    row_sum = None
    weighted = None
    for dist in range(reach + 1):
        expo_full = jnp.where(
            block_visible[dist][None], jnp.exp(block_scores[dist] - top_score[:, :, None]), 0.0
        )
        part_sum = jnp.sum(expo_full, axis=2)
        product = jnp.einsum(
            "hqk,hke->hqe",
            expo_full.astype(jnp.bfloat16),
            held[dist][1],
            preferred_element_type=jnp.float32,
        )
        row_sum = part_sum if row_sum is None else row_sum + part_sum
        weighted = product if weighted is None else weighted + product
    attended_heads = (weighted / row_sum[:, :, None]).astype(jnp.bfloat16)
    attended = row_major(attended_heads, tok_rows)
    log_sum = top_score + jnp.log(row_sum)

    upstream = out_grad[0]
    partial_weight = lax.dot_general(
        attended, upstream, (((0,), (0,)), ((), ())), preferred_element_type=jnp.float32
    )
    partial_weight, attended = lax.optimization_barrier((partial_weight, attended))
    mixed_out = jnp.dot(attended, weight_full, preferred_element_type=jnp.float32).astype(
        jnp.bfloat16
    )
    att_grad = lax.dot_general(
        upstream, weight_full, (((1,), (1,)), ((), ())), preferred_element_type=jnp.float32
    ).astype(jnp.bfloat16)

    row_share = lax.psum_scatter(
        partial_weight.astype(jnp.bfloat16), "seq", scatter_dimension=0, tiled=True
    )
    weight_grad = lax.psum_scatter(
        row_share.astype(jnp.float32), "dp", scatter_dimension=1, tiled=True
    )

    grad_heads = head_major(att_grad, tok_rows)
    delta_rows = jnp.sum(
        grad_heads.astype(jnp.float32) * attended_heads.astype(jnp.float32), axis=2
    )

    query_acc = None
    parts = [None] * (reach + 1)
    order = [d for d in range(reach, -1, -1) if d % 2 == 1] + [
        d for d in range(2, reach + 1, 2)
    ] + [0]
    for dist in order:
        key_block = held[dist][0]
        value_block = held[dist][1]
        scores = (
            jnp.einsum("hqe,hke->hqk", query_heads, key_block, preferred_element_type=jnp.float32)
            * score_scale
        )
        prob_full = jnp.where(
            block_visible[dist][None], jnp.exp(scores - log_sum[:, :, None]), 0.0
        )
        prob_back = prob_full.astype(jnp.bfloat16)
        prob_grad = jnp.einsum(
            "hqe,hke->hqk", grad_heads, value_block, preferred_element_type=jnp.float32
        )
        score_grad = (prob_full * (prob_grad - delta_rows[:, :, None])).astype(jnp.bfloat16)
        query_part = jnp.einsum(
            "hqk,hke->hqe", score_grad, key_block, preferred_element_type=jnp.float32
        )
        query_acc = query_part if query_acc is None else query_acc + query_part
        key_part = (
            jnp.einsum("hqk,hqe->hke", score_grad, query_heads, preferred_element_type=jnp.float32)
            * score_scale
        )
        value_part = jnp.einsum(
            "hqk,hqe->hke", prob_back, grad_heads, preferred_element_type=jnp.float32
        )
        parts[dist] = jnp.stack([key_part, value_part])

    kv_grad = return_behind(parts, reach, paired, core)
    query_grad = row_major(query_acc * score_scale, tok_rows).astype(jnp.bfloat16)
    key_grad = row_major(kv_grad[0], tok_rows).astype(jnp.bfloat16)
    value_grad = row_major(kv_grad[1], tok_rows).astype(jnp.bfloat16)
    return (mixed_out[None], query_grad[None], key_grad[None], value_grad[None], weight_grad)


def solution(mesh):
    return jax.shard_map(
        local,
        mesh=mesh,
        in_specs=(
            P("dp", "seq", None),
            P("dp", "seq", None),
            P("dp", "seq", None),
            P("dp", "seq", None),
            P("dp", None),
            P("seq", "dp"),
        ),
        out_specs=(
            P("dp", "seq", None),
            P("dp", "seq", None),
            P("dp", "seq", None),
            P("dp", "seq", None),
            P("seq", "dp"),
        ),
        check_vma=False,
    )
```

```python
import jax
import jax.numpy as jnp
from jax import lax
from jax.sharding import PartitionSpec as P

HEADS = 12
HEAD_DIM = 64
STRETCH = 128
MOST = 1024


MASKED_SCORE = -1e30


def shift_up(block, axis, distance):
    devices = range(lax.axis_size(axis))
    route = [(i - distance, i) for i in devices if i - distance in devices]
    return lax.ppermute(block, axis, route)


def swap_partner(block, axis):
    count = lax.axis_size(axis)
    return lax.ppermute(block, axis, [(i, i ^ 1) for i in range(count)])


def frame_labels(utt_lengths, first_frame, frame_count, total_frames):
    positions = first_frame + jnp.arange(frame_count, dtype=jnp.int32)
    utt_ends = jnp.cumsum(utt_lengths)
    utt_index = jnp.sum((positions[:, None] >= utt_ends[None, :]).astype(jnp.int32), axis=1)
    outside = (positions < 0) | (positions >= total_frames)
    return (jnp.where(outside, -1, utt_index), positions // STRETCH)


def head_major(rows, tok_rows):
    return jnp.transpose(rows.reshape(tok_rows, HEADS, HEAD_DIM), (1, 0, 2))


def row_major(heads, tok_rows):
    return jnp.transpose(heads, (1, 0, 2)).reshape(tok_rows, HEADS * HEAD_DIM)


def gather_behind(own, reach, paired, core):
    if not paired:
        held = [own]
        for _ in range(reach):
            held.append(shift_up(held[-1], "seq", 1))
        return held
    evens = {0: own}
    count = lax.axis_size("seq")
    if reach == 4 and count % 4 == 0:
        row = (lax.axis_index("seq") // 2) % 2
        later = [i for i in range(count) if (i // 2) % 2 == 1]
        earlier = [i for i in range(count) if (i // 2) % 2 == 0 and i + 2 < count]
        far = [shift_up(own[k], "seq", 4) for k in range(2)]
        near = []
        for k in range(2):
            direct = lax.ppermute(own[k], "seq", [(i - 2, i) for i in later])
            relayed = lax.ppermute(far[k], "seq", [(i + 2, i) for i in earlier])
            near.append(jnp.where(row == 1, direct, relayed))
        evens[2] = jnp.stack(near)
        evens[4] = jnp.stack(far)
    else:
        for dist in range(2, reach + 2, 2):
            evens[dist] = shift_up(own, "seq", dist)
    odds = list(range(1, reach + 1, 2))
    payload = [jnp.where(core == 0, evens[s - 1], evens[s + 1]) for s in odds]
    received = swap_partner(payload, "seq")
    held = []
    for dist in range(reach + 1):
        held.append(evens[dist] if dist % 2 == 0 else received[(dist - 1) // 2])
    return held


def return_behind(parts, reach, paired, core):
    if not paired:
        carried = parts[reach]
        for dist in range(reach - 1, -1, -1):
            carried = shift_up(carried.astype(jnp.bfloat16), "seq", -1).astype(jnp.float32) + parts[dist]
        return carried
    odds = list(range(1, reach + 1, 2))
    received = swap_partner([parts[s] for s in odds], "seq")
    summed = {}
    for dist in range(0, reach + 2, 2):
        zero = jnp.zeros_like(parts[0])
        from_core1 = received[dist // 2] if dist // 2 < len(odds) else zero
        from_core0 = received[dist // 2 - 1] if dist >= 2 and dist // 2 - 1 < len(odds) else zero
        own = parts[dist] if dist <= reach else zero
        summed[dist] = own + jnp.where(core == 0, from_core1, from_core0)
    total = summed[0]
    for dist in range(2, reach + 2, 2):
        total = total + shift_up(summed[dist].astype(jnp.bfloat16), "seq", -dist).astype(jnp.float32)
    return total


def local(query_rows, key_rows, value_rows, out_grad, lengths, out_weight):
    seq_count = lax.axis_size("seq")
    device = lax.axis_index("seq")
    core = device % 2
    paired = seq_count % 2 == 0
    tok_rows = query_rows.shape[1]
    feature_width = query_rows.shape[2]
    total_frames = seq_count * tok_rows
    reach = min(-(-MOST // tok_rows), seq_count - 1)
    score_scale = HEAD_DIM ** (-0.5)
    utt_lengths = lengths[0]

    row_blocks, col_blocks = lax.axis_size("seq"), lax.axis_size("dp")
    pieces = lax.all_gather(out_weight, ("seq", "dp"), axis=0, tiled=False)
    weight_full = jnp.transpose(
        pieces.reshape((row_blocks, col_blocks) + out_weight.shape), (0, 2, 1, 3)
    ).reshape(row_blocks * out_weight.shape[0], col_blocks * out_weight.shape[1])

    query_heads = head_major(query_rows[0], tok_rows)
    own_kv = jnp.stack([head_major(key_rows[0], tok_rows), head_major(value_rows[0], tok_rows)])
    held = gather_behind(own_kv, reach, paired, core)

    query_utt, query_stretch = frame_labels(utt_lengths, device * tok_rows, tok_rows, total_frames)
    block_visible = []
    for dist in range(reach + 1):
        key_utt, key_stretch = frame_labels(
            utt_lengths, (device - dist) * tok_rows, tok_rows, total_frames
        )
        block_visible.append(
            (query_utt[:, None] == key_utt[None, :]) & (key_stretch[None, :] <= query_stretch[:, None])
        )

    block_scores = []
    top_score = None
    for dist in range(reach + 1):
        scores = (
            jnp.einsum("hqe,hke->hqk", query_heads, held[dist][0], preferred_element_type=jnp.float32)
            * score_scale
        )
        scores = jnp.where(block_visible[dist][None], scores, MASKED_SCORE)
        block_scores.append(scores)
        block_top = jnp.max(scores, axis=2)
        top_score = block_top if top_score is None else jnp.maximum(top_score, block_top)
    row_sum = None
    weighted = None
    for dist in range(reach + 1):
        expo_full = jnp.where(
            block_visible[dist][None], jnp.exp(block_scores[dist] - top_score[:, :, None]), 0.0
        )
        part_sum = jnp.sum(expo_full, axis=2)
        product = jnp.einsum(
            "hqk,hke->hqe",
            expo_full.astype(jnp.bfloat16),
            held[dist][1],
            preferred_element_type=jnp.float32,
        )
        row_sum = part_sum if row_sum is None else row_sum + part_sum
        weighted = product if weighted is None else weighted + product
    attended_heads = (weighted / row_sum[:, :, None]).astype(jnp.bfloat16)
    attended = row_major(attended_heads, tok_rows)
    log_sum = top_score + jnp.log(row_sum)

    upstream = out_grad[0]
    partial_weight = lax.dot_general(
        attended, upstream, (((0,), (0,)), ((), ())), preferred_element_type=jnp.float32
    )
    partial_weight, attended = lax.optimization_barrier((partial_weight, attended))
    mixed_out = jnp.dot(attended, weight_full, preferred_element_type=jnp.float32).astype(
        jnp.bfloat16
    )
    att_grad = lax.dot_general(
        upstream, weight_full, (((1,), (1,)), ((), ())), preferred_element_type=jnp.float32
    ).astype(jnp.bfloat16)

    row_share = lax.psum_scatter(
        partial_weight.astype(jnp.bfloat16), "seq", scatter_dimension=0, tiled=True
    )
    weight_grad = lax.psum_scatter(
        row_share.astype(jnp.float32), "dp", scatter_dimension=1, tiled=True
    )

    grad_heads = head_major(att_grad, tok_rows)
    delta_rows = jnp.sum(
        grad_heads.astype(jnp.float32) * attended_heads.astype(jnp.float32), axis=2
    )

    query_acc = None
    parts = [None] * (reach + 1)
    order = [d for d in range(reach, -1, -1) if d % 2 == 1] + [
        d for d in range(2, reach + 1, 2)
    ] + [0]
    for dist in order:
        key_block = held[dist][0]
        value_block = held[dist][1]
        scores = (
            jnp.einsum("hqe,hke->hqk", query_heads, key_block, preferred_element_type=jnp.float32)
            * score_scale
        )
        prob_full = jnp.where(
            block_visible[dist][None], jnp.exp(scores - log_sum[:, :, None]), 0.0
        )
        prob_back = prob_full.astype(jnp.bfloat16)
        prob_grad = jnp.einsum(
            "hqe,hke->hqk", grad_heads, value_block, preferred_element_type=jnp.float32
        )
        score_grad = (prob_full * (prob_grad - delta_rows[:, :, None])).astype(jnp.bfloat16)
        query_part = jnp.einsum(
            "hqk,hke->hqe", score_grad, key_block, preferred_element_type=jnp.float32
        )
        query_acc = query_part if query_acc is None else query_acc + query_part
        key_part = (
            jnp.einsum("hqk,hqe->hke", score_grad, query_heads, preferred_element_type=jnp.float32)
            * score_scale
        )
        value_part = jnp.einsum(
            "hqk,hqe->hke", prob_back, grad_heads, preferred_element_type=jnp.float32
        )
        parts[dist] = jnp.stack([key_part, value_part])

    kv_grad = return_behind(parts, reach, paired, core)
    query_grad = row_major(query_acc * score_scale, tok_rows).astype(jnp.bfloat16)
    key_grad = row_major(kv_grad[0], tok_rows).astype(jnp.bfloat16)
    value_grad = row_major(kv_grad[1], tok_rows).astype(jnp.bfloat16)
    return (mixed_out[None], query_grad[None], key_grad[None], value_grad[None], weight_grad)


def solution(mesh):
    return jax.shard_map(
        local,
        mesh=mesh,
        in_specs=(
            P("dp", "seq", None),
            P("dp", "seq", None),
            P("dp", "seq", None),
            P("dp", "seq", None),
            P("dp", None),
            P("seq", "dp"),
        ),
        out_specs=(
            P("dp", "seq", None),
            P("dp", "seq", None),
            P("dp", "seq", None),
            P("dp", "seq", None),
            P("seq", "dp"),
        ),
        check_vma=False,
    )
```

```python
import jax
import jax.numpy as jnp
from jax import lax
from jax.sharding import PartitionSpec as P

HEADS = 12
HEAD_DIM = 64
STRETCH = 128
MOST = 1024


MASKED_SCORE = -1e30


SEQ = ("chip", "core")


def axis_count(axis):
    if isinstance(axis, tuple):
        count = 1
        for name in axis:
            count *= lax.axis_size(name)
        return count
    return lax.axis_size(axis)


def shift_up(block, axis, distance):
    devices = range(axis_count(axis))
    route = [(i - distance, i) for i in devices if i - distance in devices]
    return lax.ppermute(block, axis, route)


def swap_partner(block, axis):
    return lax.ppermute(block, "core", [(0, 1), (1, 0)])


def frame_labels(utt_lengths, first_frame, frame_count, total_frames):
    positions = first_frame + jnp.arange(frame_count, dtype=jnp.int32)
    utt_ends = jnp.cumsum(utt_lengths)
    utt_index = jnp.sum((positions[:, None] >= utt_ends[None, :]).astype(jnp.int32), axis=1)
    outside = (positions < 0) | (positions >= total_frames)
    return (jnp.where(outside, -1, utt_index), positions // STRETCH)


def head_major(rows, tok_rows):
    return jnp.transpose(rows.reshape(tok_rows, HEADS, HEAD_DIM), (1, 0, 2))


def row_major(heads, tok_rows):
    return jnp.transpose(heads, (1, 0, 2)).reshape(tok_rows, HEADS * HEAD_DIM)


def gather_behind(own, reach, paired, core):
    if not paired:
        held = [own]
        for _ in range(reach):
            held.append(shift_up(held[-1], SEQ, 1))
        return held
    evens = {0: own}
    count = axis_count(SEQ)
    if reach == 4 and count % 4 == 0:
        row = (lax.axis_index(SEQ) // 2) % 2
        later = [i for i in range(count) if (i // 2) % 2 == 1]
        earlier = [i for i in range(count) if (i // 2) % 2 == 0 and i + 2 < count]
        far = [shift_up(own[k], SEQ, 4) for k in range(2)]
        near = []
        for k in range(2):
            direct = lax.ppermute(own[k], SEQ, [(i - 2, i) for i in later])
            relayed = lax.ppermute(far[k], SEQ, [(i + 2, i) for i in earlier])
            near.append(jnp.where(row == 1, direct, relayed))
        evens[2] = jnp.stack(near)
        evens[4] = jnp.stack(far)
    else:
        for dist in range(2, reach + 2, 2):
            evens[dist] = shift_up(own, SEQ, dist)
    odds = list(range(1, reach + 1, 2))
    payload = [jnp.where(core == 0, evens[s - 1], evens[s + 1]) for s in odds]
    received = swap_partner(payload, SEQ)
    held = []
    for dist in range(reach + 1):
        held.append(evens[dist] if dist % 2 == 0 else received[(dist - 1) // 2])
    return held


def return_behind(parts, reach, paired, core):
    if not paired:
        carried = parts[reach]
        for dist in range(reach - 1, -1, -1):
            carried = shift_up(carried.astype(jnp.bfloat16), SEQ, -1).astype(jnp.float32) + parts[dist]
        return carried
    odds = list(range(1, reach + 1, 2))
    received = swap_partner([parts[s] for s in odds], SEQ)
    summed = {}
    for dist in range(0, reach + 2, 2):
        zero = jnp.zeros_like(parts[0])
        from_core1 = received[dist // 2] if dist // 2 < len(odds) else zero
        from_core0 = received[dist // 2 - 1] if dist >= 2 and dist // 2 - 1 < len(odds) else zero
        own = parts[dist] if dist <= reach else zero
        summed[dist] = own + jnp.where(core == 0, from_core1, from_core0)
    count = axis_count(SEQ)
    if reach == 4 and count % 4 == 0:
        row = (lax.axis_index(SEQ) // 2) % 2
        later = [i for i in range(count) if (i // 2) % 2 == 1]
        earlier = [i for i in range(count) if (i // 2) % 2 == 0 and i + 2 < count]
        near = summed[2].astype(jnp.bfloat16)
        direct = lax.ppermute(near, SEQ, [(i, i - 2) for i in later])
        relayed = lax.ppermute(near, SEQ, [(i, i + 2) for i in earlier])
        far = summed[4] + jnp.where(row == 1, relayed.astype(jnp.float32), 0.0)
        total = summed[0] + jnp.where(row == 0, direct.astype(jnp.float32), 0.0)
        return total + shift_up(far.astype(jnp.bfloat16), SEQ, -4).astype(jnp.float32)
    total = summed[0]
    for dist in range(2, reach + 2, 2):
        total = total + shift_up(summed[dist].astype(jnp.bfloat16), SEQ, -dist).astype(jnp.float32)
    return total


def local(query_rows, key_rows, value_rows, out_grad, lengths, out_weight):
    seq_count = axis_count(SEQ)
    device = lax.axis_index(SEQ)
    core = lax.axis_index("core")
    paired = True
    tok_rows = query_rows.shape[1]
    feature_width = query_rows.shape[2]
    total_frames = seq_count * tok_rows
    reach = min(-(-MOST // tok_rows), seq_count - 1)
    score_scale = HEAD_DIM ** (-0.5)
    utt_lengths = lengths[0]

    row_blocks, col_blocks = axis_count(SEQ), lax.axis_size("dp")
    pieces = lax.all_gather(out_weight, SEQ + ("dp",), axis=0, tiled=False)
    weight_full = jnp.transpose(
        pieces.reshape((row_blocks, col_blocks) + out_weight.shape), (0, 2, 1, 3)
    ).reshape(row_blocks * out_weight.shape[0], col_blocks * out_weight.shape[1])

    query_heads = head_major(query_rows[0], tok_rows)
    own_kv = jnp.stack([head_major(key_rows[0], tok_rows), head_major(value_rows[0], tok_rows)])
    held = gather_behind(own_kv, reach, paired, core)

    query_utt, query_stretch = frame_labels(utt_lengths, device * tok_rows, tok_rows, total_frames)
    block_visible = []
    for dist in range(reach + 1):
        key_utt, key_stretch = frame_labels(
            utt_lengths, (device - dist) * tok_rows, tok_rows, total_frames
        )
        block_visible.append(
            (query_utt[:, None] == key_utt[None, :]) & (key_stretch[None, :] <= query_stretch[:, None])
        )

    block_scores = []
    top_score = None
    for dist in range(reach + 1):
        scores = (
            jnp.einsum("hqe,hke->hqk", query_heads, held[dist][0], preferred_element_type=jnp.float32)
            * score_scale
        )
        scores = jnp.where(block_visible[dist][None], scores, MASKED_SCORE)
        block_scores.append(scores)
        block_top = jnp.max(scores, axis=2)
        top_score = block_top if top_score is None else jnp.maximum(top_score, block_top)
    row_sum = None
    weighted = None
    for dist in range(reach + 1):
        expo_full = jnp.where(
            block_visible[dist][None], jnp.exp(block_scores[dist] - top_score[:, :, None]), 0.0
        )
        part_sum = jnp.sum(expo_full, axis=2)
        product = jnp.einsum(
            "hqk,hke->hqe",
            expo_full.astype(jnp.bfloat16),
            held[dist][1],
            preferred_element_type=jnp.float32,
        )
        row_sum = part_sum if row_sum is None else row_sum + part_sum
        weighted = product if weighted is None else weighted + product
    attended_heads = (weighted / row_sum[:, :, None]).astype(jnp.bfloat16)
    attended = row_major(attended_heads, tok_rows)
    log_sum = top_score + jnp.log(row_sum)

    upstream = out_grad[0]
    partial_weight = lax.dot_general(
        attended, upstream, (((0,), (0,)), ((), ())), preferred_element_type=jnp.float32
    )
    partial_weight, attended = lax.optimization_barrier((partial_weight, attended))
    mixed_out = jnp.dot(attended, weight_full, preferred_element_type=jnp.float32).astype(
        jnp.bfloat16
    )
    att_grad = lax.dot_general(
        upstream, weight_full, (((1,), (1,)), ((), ())), preferred_element_type=jnp.float32
    ).astype(jnp.bfloat16)

    chip_count = lax.axis_size("chip")
    halves = partial_weight.reshape(chip_count, 2, -1, partial_weight.shape[1])
    keep = lax.dynamic_index_in_dim(halves, core, 1, keepdims=False)
    give = lax.dynamic_index_in_dim(halves, 1 - core, 1, keepdims=False)
    core_sum = keep + swap_partner(give, SEQ)
    row_share = lax.psum_scatter(
        core_sum.reshape(-1, partial_weight.shape[1]).astype(jnp.bfloat16),
        "chip",
        scatter_dimension=0,
        tiled=True,
    )
    weight_grad = lax.psum_scatter(
        row_share.astype(jnp.float32), "dp", scatter_dimension=1, tiled=True
    )

    grad_heads = head_major(att_grad, tok_rows)
    delta_rows = jnp.sum(
        grad_heads.astype(jnp.float32) * attended_heads.astype(jnp.float32), axis=2
    )

    query_acc = None
    parts = [None] * (reach + 1)
    order = [d for d in range(reach, -1, -1) if d % 2 == 1] + [
        d for d in range(2, reach + 1, 2)
    ] + [0]
    for dist in order:
        key_block = held[dist][0]
        value_block = held[dist][1]
        scores = (
            jnp.einsum("hqe,hke->hqk", query_heads, key_block, preferred_element_type=jnp.float32)
            * score_scale
        )
        prob_full = jnp.where(
            block_visible[dist][None], jnp.exp(scores - log_sum[:, :, None]), 0.0
        )
        prob_back = prob_full.astype(jnp.bfloat16)
        prob_grad = jnp.einsum(
            "hqe,hke->hqk", grad_heads, value_block, preferred_element_type=jnp.float32
        )
        score_grad = (prob_full * (prob_grad - delta_rows[:, :, None])).astype(jnp.bfloat16)
        query_part = jnp.einsum(
            "hqk,hke->hqe", score_grad, key_block, preferred_element_type=jnp.float32
        )
        query_acc = query_part if query_acc is None else query_acc + query_part
        key_part = (
            jnp.einsum("hqk,hqe->hke", score_grad, query_heads, preferred_element_type=jnp.float32)
            * score_scale
        )
        value_part = jnp.einsum(
            "hqk,hqe->hke", prob_back, grad_heads, preferred_element_type=jnp.float32
        )
        parts[dist] = jnp.stack([key_part, value_part])

    kv_grad = return_behind(parts, reach, paired, core)
    query_grad = row_major(query_acc * score_scale, tok_rows).astype(jnp.bfloat16)
    key_grad = row_major(kv_grad[0], tok_rows).astype(jnp.bfloat16)
    value_grad = row_major(kv_grad[1], tok_rows).astype(jnp.bfloat16)
    return (mixed_out[None], query_grad[None], key_grad[None], value_grad[None], weight_grad)


def solution(mesh):
    names = list(mesh.axis_names)
    at = names.index("seq")
    shape = mesh.devices.shape
    split_mesh = jax.sharding.Mesh(
        mesh.devices.reshape(shape[:at] + (shape[at] // 2, 2) + shape[at + 1 :]),
        tuple(names[:at] + ["chip", "core"] + names[at + 1 :]),
    )
    return jax.shard_map(
        local,
        mesh=split_mesh,
        in_specs=(
            P("dp", SEQ, None),
            P("dp", SEQ, None),
            P("dp", SEQ, None),
            P("dp", SEQ, None),
            P("dp", None),
            P(SEQ, "dp"),
        ),
        out_specs=(
            P("dp", SEQ, None),
            P("dp", SEQ, None),
            P("dp", SEQ, None),
            P("dp", SEQ, None),
            P(SEQ, "dp"),
        ),
        check_vma=False,
    )
```

```python
import jax
import jax.numpy as jnp
from jax import lax
from jax.sharding import PartitionSpec as P

HEADS = 12
HEAD_DIM = 64
STRETCH = 128
MOST = 1024


MASKED_SCORE = -1e30


def shift_up(block, axis, distance):
    devices = range(lax.axis_size(axis))
    route = [(i - distance, i) for i in devices if i - distance in devices]
    return lax.ppermute(block, axis, route)


def swap_partner(block, axis):
    count = lax.axis_size(axis)
    return lax.ppermute(block, axis, [(i, i ^ 1) for i in range(count)])


def frame_labels(utt_lengths, first_frame, frame_count, total_frames):
    positions = first_frame + jnp.arange(frame_count, dtype=jnp.int32)
    utt_ends = jnp.cumsum(utt_lengths)
    utt_index = jnp.sum((positions[:, None] >= utt_ends[None, :]).astype(jnp.int32), axis=1)
    outside = (positions < 0) | (positions >= total_frames)
    return (jnp.where(outside, -1, utt_index), positions // STRETCH)


def head_major(rows, tok_rows):
    return jnp.transpose(rows.reshape(tok_rows, HEADS, HEAD_DIM), (1, 0, 2))


def row_major(heads, tok_rows):
    return jnp.transpose(heads, (1, 0, 2)).reshape(tok_rows, HEADS * HEAD_DIM)


def gather_behind(own, reach, paired, core):
    if not paired:
        held = [own]
        for _ in range(reach):
            held.append(shift_up(held[-1], "seq", 1))
        return held
    evens = {0: own}
    count = lax.axis_size("seq")
    if reach == 4 and count % 4 == 0:
        row = (lax.axis_index("seq") // 2) % 2
        later = [i for i in range(count) if (i // 2) % 2 == 1]
        earlier = [i for i in range(count) if (i // 2) % 2 == 0 and i + 2 < count]
        far = shift_up(own, "seq", 4)
        direct = lax.ppermute(own, "seq", [(i - 2, i) for i in later])
        relayed = lax.ppermute(far, "seq", [(i + 2, i) for i in earlier])
        evens[2] = jnp.where(row == 1, direct, relayed)
        evens[4] = far
    else:
        for dist in range(2, reach + 2, 2):
            evens[dist] = shift_up(own, "seq", dist)
    odds = list(range(1, reach + 1, 2))
    payload = [jnp.where(core == 0, evens[s - 1], evens[s + 1]) for s in odds]
    received = swap_partner(payload, "seq")
    held = []
    for dist in range(reach + 1):
        held.append(evens[dist] if dist % 2 == 0 else received[(dist - 1) // 2])
    return held


def return_behind(parts, reach, paired, core):
    if not paired:
        carried = parts[reach]
        for dist in range(reach - 1, -1, -1):
            carried = shift_up(carried.astype(jnp.bfloat16), "seq", -1).astype(jnp.float32) + parts[dist]
        return carried
    odds = list(range(1, reach + 1, 2))
    received = swap_partner([parts[s] for s in odds], "seq")
    summed = {}
    for dist in range(0, reach + 2, 2):
        zero = jnp.zeros_like(parts[0])
        from_core1 = received[dist // 2] if dist // 2 < len(odds) else zero
        from_core0 = received[dist // 2 - 1] if dist >= 2 and dist // 2 - 1 < len(odds) else zero
        own = parts[dist] if dist <= reach else zero
        summed[dist] = own + jnp.where(core == 0, from_core1, from_core0)
    count = lax.axis_size("seq")
    if reach == 4 and count % 4 == 0:
        row = (lax.axis_index("seq") // 2) % 2
        later = [i for i in range(count) if (i // 2) % 2 == 1]
        earlier = [i for i in range(count) if (i // 2) % 2 == 0 and i + 2 < count]
        near = summed[2].astype(jnp.bfloat16)
        direct = lax.ppermute(near, "seq", [(i, i - 2) for i in later])
        relayed = lax.ppermute(near, "seq", [(i, i + 2) for i in earlier])
        far = summed[4] + jnp.where(row == 1, relayed.astype(jnp.float32), 0.0)
        total = summed[0] + jnp.where(row == 0, direct.astype(jnp.float32), 0.0)
        return total + shift_up(far.astype(jnp.bfloat16), "seq", -4).astype(jnp.float32)
    total = summed[0]
    for dist in range(2, reach + 2, 2):
        total = total + shift_up(summed[dist].astype(jnp.bfloat16), "seq", -dist).astype(jnp.float32)
    return total


def local(query_rows, key_rows, value_rows, out_grad, lengths, out_weight):
    seq_count = lax.axis_size("seq")
    device = lax.axis_index("seq")
    core = device % 2
    paired = seq_count % 2 == 0
    tok_rows = query_rows.shape[1]
    feature_width = query_rows.shape[2]
    total_frames = seq_count * tok_rows
    reach = min(-(-MOST // tok_rows), seq_count - 1)
    score_scale = HEAD_DIM ** (-0.5)
    utt_lengths = lengths[0]

    row_blocks, col_blocks = lax.axis_size("seq"), lax.axis_size("dp")
    pieces = lax.all_gather(out_weight, ("seq", "dp"), axis=0, tiled=False)
    weight_full = jnp.transpose(
        pieces.reshape((row_blocks, col_blocks) + out_weight.shape), (0, 2, 1, 3)
    ).reshape(row_blocks * out_weight.shape[0], col_blocks * out_weight.shape[1])

    query_heads = head_major(query_rows[0], tok_rows)
    own_kv = jnp.stack([head_major(key_rows[0], tok_rows), head_major(value_rows[0], tok_rows)])
    held = gather_behind(own_kv, reach, paired, core)

    query_utt, query_stretch = frame_labels(utt_lengths, device * tok_rows, tok_rows, total_frames)
    block_visible = []
    for dist in range(reach + 1):
        key_utt, key_stretch = frame_labels(
            utt_lengths, (device - dist) * tok_rows, tok_rows, total_frames
        )
        block_visible.append(
            (query_utt[:, None] == key_utt[None, :]) & (key_stretch[None, :] <= query_stretch[:, None])
        )

    block_scores = []
    top_score = None
    for dist in range(reach + 1):
        scores = (
            jnp.einsum("hqe,hke->hqk", query_heads, held[dist][0], preferred_element_type=jnp.float32)
            * score_scale
        )
        scores = jnp.where(block_visible[dist][None], scores, MASKED_SCORE)
        block_scores.append(scores)
        block_top = jnp.max(scores, axis=2)
        top_score = block_top if top_score is None else jnp.maximum(top_score, block_top)
    row_sum = None
    weighted = None
    for dist in range(reach + 1):
        expo_full = jnp.where(
            block_visible[dist][None], jnp.exp(block_scores[dist] - top_score[:, :, None]), 0.0
        )
        part_sum = jnp.sum(expo_full, axis=2)
        product = jnp.einsum(
            "hqk,hke->hqe",
            expo_full.astype(jnp.bfloat16),
            held[dist][1],
            preferred_element_type=jnp.float32,
        )
        row_sum = part_sum if row_sum is None else row_sum + part_sum
        weighted = product if weighted is None else weighted + product
    attended_heads = (weighted / row_sum[:, :, None]).astype(jnp.bfloat16)
    attended = row_major(attended_heads, tok_rows)
    log_sum = top_score + jnp.log(row_sum)

    upstream = out_grad[0]
    partial_weight = lax.dot_general(
        attended, upstream, (((0,), (0,)), ((), ())), preferred_element_type=jnp.float32
    )
    partial_weight, attended = lax.optimization_barrier((partial_weight, attended))
    mixed_out = jnp.dot(attended, weight_full, preferred_element_type=jnp.float32).astype(
        jnp.bfloat16
    )
    att_grad = lax.dot_general(
        upstream, weight_full, (((1,), (1,)), ((), ())), preferred_element_type=jnp.float32
    ).astype(jnp.bfloat16)

    row_share = lax.psum_scatter(
        partial_weight.astype(jnp.bfloat16), "seq", scatter_dimension=0, tiled=True
    )
    weight_grad = lax.psum_scatter(
        row_share.astype(jnp.float32), "dp", scatter_dimension=1, tiled=True
    )

    grad_heads = head_major(att_grad, tok_rows)
    delta_rows = jnp.sum(
        grad_heads.astype(jnp.float32) * attended_heads.astype(jnp.float32), axis=2
    )

    query_acc = None
    parts = [None] * (reach + 1)
    order = [d for d in range(reach, -1, -1) if d % 2 == 1] + [
        d for d in range(2, reach + 1, 2)
    ] + [0]
    for dist in order:
        key_block = held[dist][0]
        value_block = held[dist][1]
        scores = (
            jnp.einsum("hqe,hke->hqk", query_heads, key_block, preferred_element_type=jnp.float32)
            * score_scale
        )
        prob_full = jnp.where(
            block_visible[dist][None], jnp.exp(scores - log_sum[:, :, None]), 0.0
        )
        prob_back = prob_full.astype(jnp.bfloat16)
        prob_grad = jnp.einsum(
            "hqe,hke->hqk", grad_heads, value_block, preferred_element_type=jnp.float32
        )
        score_grad = (prob_full * (prob_grad - delta_rows[:, :, None])).astype(jnp.bfloat16)
        query_part = jnp.einsum(
            "hqk,hke->hqe", score_grad, key_block, preferred_element_type=jnp.float32
        )
        query_acc = query_part if query_acc is None else query_acc + query_part
        key_part = (
            jnp.einsum("hqk,hqe->hke", score_grad, query_heads, preferred_element_type=jnp.float32)
            * score_scale
        )
        value_part = jnp.einsum(
            "hqk,hqe->hke", prob_back, grad_heads, preferred_element_type=jnp.float32
        )
        parts[dist] = jnp.stack([key_part, value_part])

    kv_grad = return_behind(parts, reach, paired, core)
    query_grad = row_major(query_acc * score_scale, tok_rows).astype(jnp.bfloat16)
    key_grad = row_major(kv_grad[0], tok_rows).astype(jnp.bfloat16)
    value_grad = row_major(kv_grad[1], tok_rows).astype(jnp.bfloat16)
    return (mixed_out[None], query_grad[None], key_grad[None], value_grad[None], weight_grad)


def solution(mesh):
    return jax.shard_map(
        local,
        mesh=mesh,
        in_specs=(
            P("dp", "seq", None),
            P("dp", "seq", None),
            P("dp", "seq", None),
            P("dp", "seq", None),
            P("dp", None),
            P("seq", "dp"),
        ),
        out_specs=(
            P("dp", "seq", None),
            P("dp", "seq", None),
            P("dp", "seq", None),
            P("dp", "seq", None),
            P("seq", "dp"),
        ),
        check_vma=False,
    )
```

```python
import jax
import jax.numpy as jnp
from jax import lax
from jax.sharding import PartitionSpec as P

HEADS = 12
HEAD_DIM = 64
STRETCH = 128
MOST = 1024


MASKED_SCORE = -1e30


def shift_up(block, axis, distance):
    devices = range(lax.axis_size(axis))
    route = [(i - distance, i) for i in devices if i - distance in devices]
    return lax.ppermute(block, axis, route)


def swap_partner(block, axis):
    count = lax.axis_size(axis)
    return lax.ppermute(block, axis, [(i, i ^ 1) for i in range(count)])


def frame_labels(utt_lengths, first_frame, frame_count, total_frames):
    positions = first_frame + jnp.arange(frame_count, dtype=jnp.int32)
    utt_ends = jnp.cumsum(utt_lengths)
    utt_index = jnp.sum((positions[:, None] >= utt_ends[None, :]).astype(jnp.int32), axis=1)
    outside = (positions < 0) | (positions >= total_frames)
    return (jnp.where(outside, -1, utt_index), positions // STRETCH)


def head_major(rows, tok_rows):
    return jnp.transpose(rows.reshape(tok_rows, HEADS, HEAD_DIM), (1, 0, 2))


def row_major(heads, tok_rows):
    return jnp.transpose(heads, (1, 0, 2)).reshape(tok_rows, HEADS * HEAD_DIM)


def gather_behind(own, reach, paired, core):
    if not paired:
        held = [own]
        for _ in range(reach):
            held.append(shift_up(held[-1], "seq", 1))
        return held
    evens = {0: own}
    count = lax.axis_size("seq")
    if reach == 4 and count % 4 == 0:
        row = (lax.axis_index("seq") // 2) % 2
        later = [i for i in range(count) if (i // 2) % 2 == 1]
        earlier = [i for i in range(count) if (i // 2) % 2 == 0 and i + 2 < count]
        far = [shift_up(own[k], "seq", 4) for k in range(2)]
        near = []
        for k in range(2):
            direct = lax.ppermute(own[k], "seq", [(i - 2, i) for i in later])
            relayed = lax.ppermute(far[k], "seq", [(i + 2, i) for i in earlier])
            near.append(jnp.where(row == 1, direct, relayed))
        evens[2] = jnp.stack(near)
        evens[4] = jnp.stack(far)
    else:
        for dist in range(2, reach + 2, 2):
            evens[dist] = shift_up(own, "seq", dist)
    odds = list(range(1, reach + 1, 2))
    payload = [jnp.where(core == 0, evens[s - 1], evens[s + 1]) for s in odds]
    received = swap_partner(payload, "seq")
    held = []
    for dist in range(reach + 1):
        held.append(evens[dist] if dist % 2 == 0 else received[(dist - 1) // 2])
    return held


def return_behind(parts, reach, paired, core):
    if not paired:
        carried = parts[reach]
        for dist in range(reach - 1, -1, -1):
            carried = shift_up(carried.astype(jnp.bfloat16), "seq", -1).astype(jnp.float32) + parts[dist]
        return carried
    odds = list(range(1, reach + 1, 2))
    received = swap_partner([parts[s] for s in odds], "seq")
    summed = {}
    for dist in range(0, reach + 2, 2):
        zero = jnp.zeros_like(parts[0])
        from_core1 = received[dist // 2] if dist // 2 < len(odds) else zero
        from_core0 = received[dist // 2 - 1] if dist >= 2 and dist // 2 - 1 < len(odds) else zero
        own = parts[dist] if dist <= reach else zero
        summed[dist] = own + jnp.where(core == 0, from_core1, from_core0)
    count = lax.axis_size("seq")
    if reach == 4 and count % 4 == 0:
        row = (lax.axis_index("seq") // 2) % 2
        later = [i for i in range(count) if (i // 2) % 2 == 1]
        earlier = [i for i in range(count) if (i // 2) % 2 == 0 and i + 2 < count]
        pieces = []
        for k in range(2):
            near = summed[2][k].astype(jnp.bfloat16)
            direct = lax.ppermute(near, "seq", [(i, i - 2) for i in later])
            relayed = lax.ppermute(near, "seq", [(i, i + 2) for i in earlier])
            far = summed[4][k] + jnp.where(row == 1, relayed.astype(jnp.float32), 0.0)
            piece = summed[0][k] + jnp.where(row == 0, direct.astype(jnp.float32), 0.0)
            pieces.append(piece + shift_up(far.astype(jnp.bfloat16), "seq", -4).astype(jnp.float32))
        return jnp.stack(pieces)
    total = summed[0]
    for dist in range(2, reach + 2, 2):
        total = total + shift_up(summed[dist].astype(jnp.bfloat16), "seq", -dist).astype(jnp.float32)
    return total


def local(query_rows, key_rows, value_rows, out_grad, lengths, out_weight):
    seq_count = lax.axis_size("seq")
    device = lax.axis_index("seq")
    core = device % 2
    paired = seq_count % 2 == 0
    tok_rows = query_rows.shape[1]
    feature_width = query_rows.shape[2]
    total_frames = seq_count * tok_rows
    reach = min(-(-MOST // tok_rows), seq_count - 1)
    score_scale = HEAD_DIM ** (-0.5)
    utt_lengths = lengths[0]

    row_blocks, col_blocks = lax.axis_size("seq"), lax.axis_size("dp")
    pieces = lax.all_gather(out_weight, ("seq", "dp"), axis=0, tiled=False)
    weight_full = jnp.transpose(
        pieces.reshape((row_blocks, col_blocks) + out_weight.shape), (0, 2, 1, 3)
    ).reshape(row_blocks * out_weight.shape[0], col_blocks * out_weight.shape[1])

    query_heads = head_major(query_rows[0], tok_rows)
    own_kv = jnp.stack([head_major(key_rows[0], tok_rows), head_major(value_rows[0], tok_rows)])
    held = gather_behind(own_kv, reach, paired, core)

    query_utt, query_stretch = frame_labels(utt_lengths, device * tok_rows, tok_rows, total_frames)
    block_visible = []
    for dist in range(reach + 1):
        key_utt, key_stretch = frame_labels(
            utt_lengths, (device - dist) * tok_rows, tok_rows, total_frames
        )
        block_visible.append(
            (query_utt[:, None] == key_utt[None, :]) & (key_stretch[None, :] <= query_stretch[:, None])
        )

    block_scores = []
    top_score = None
    for dist in range(reach + 1):
        scores = (
            jnp.einsum("hqe,hke->hqk", query_heads, held[dist][0], preferred_element_type=jnp.float32)
            * score_scale
        )
        scores = jnp.where(block_visible[dist][None], scores, MASKED_SCORE)
        block_scores.append(scores)
        block_top = jnp.max(scores, axis=2)
        top_score = block_top if top_score is None else jnp.maximum(top_score, block_top)
    row_sum = None
    weighted = None
    for dist in range(reach + 1):
        expo_full = jnp.where(
            block_visible[dist][None], jnp.exp(block_scores[dist] - top_score[:, :, None]), 0.0
        )
        part_sum = jnp.sum(expo_full, axis=2)
        product = jnp.einsum(
            "hqk,hke->hqe",
            expo_full.astype(jnp.bfloat16),
            held[dist][1],
            preferred_element_type=jnp.float32,
        )
        row_sum = part_sum if row_sum is None else row_sum + part_sum
        weighted = product if weighted is None else weighted + product
    attended_heads = (weighted / row_sum[:, :, None]).astype(jnp.bfloat16)
    attended = row_major(attended_heads, tok_rows)
    log_sum = top_score + jnp.log(row_sum)

    upstream = out_grad[0]
    partial_weight = lax.dot_general(
        attended, upstream, (((0,), (0,)), ((), ())), preferred_element_type=jnp.float32
    )
    partial_weight, attended = lax.optimization_barrier((partial_weight, attended))
    mixed_out = jnp.dot(attended, weight_full, preferred_element_type=jnp.float32).astype(
        jnp.bfloat16
    )
    att_grad = lax.dot_general(
        upstream, weight_full, (((1,), (1,)), ((), ())), preferred_element_type=jnp.float32
    ).astype(jnp.bfloat16)

    row_share = lax.psum_scatter(
        partial_weight.astype(jnp.bfloat16), "seq", scatter_dimension=0, tiled=True
    )
    weight_grad = lax.psum_scatter(
        row_share.astype(jnp.float32), "dp", scatter_dimension=1, tiled=True
    )

    grad_heads = head_major(att_grad, tok_rows)
    delta_rows = jnp.sum(
        grad_heads.astype(jnp.float32) * attended_heads.astype(jnp.float32), axis=2
    )

    query_acc = None
    parts = [None] * (reach + 1)
    order = [d for d in range(reach, -1, -1) if d % 2 == 1] + [
        d for d in range(2, reach + 1, 2)
    ] + [0]
    for dist in order:
        key_block = held[dist][0]
        value_block = held[dist][1]
        scores = (
            jnp.einsum("hqe,hke->hqk", query_heads, key_block, preferred_element_type=jnp.float32)
            * score_scale
        )
        prob_full = jnp.where(
            block_visible[dist][None], jnp.exp(scores - log_sum[:, :, None]), 0.0
        )
        prob_back = prob_full.astype(jnp.bfloat16)
        prob_grad = jnp.einsum(
            "hqe,hke->hqk", grad_heads, value_block, preferred_element_type=jnp.float32
        )
        score_grad = (prob_full * (prob_grad - delta_rows[:, :, None])).astype(jnp.bfloat16)
        query_part = jnp.einsum(
            "hqk,hke->hqe", score_grad, key_block, preferred_element_type=jnp.float32
        )
        query_acc = query_part if query_acc is None else query_acc + query_part
        key_part = (
            jnp.einsum("hqk,hqe->hke", score_grad, query_heads, preferred_element_type=jnp.float32)
            * score_scale
        )
        value_part = jnp.einsum(
            "hqk,hqe->hke", prob_back, grad_heads, preferred_element_type=jnp.float32
        )
        parts[dist] = jnp.stack([key_part, value_part])

    kv_grad = return_behind(parts, reach, paired, core)
    query_grad = row_major(query_acc * score_scale, tok_rows).astype(jnp.bfloat16)
    key_grad = row_major(kv_grad[0], tok_rows).astype(jnp.bfloat16)
    value_grad = row_major(kv_grad[1], tok_rows).astype(jnp.bfloat16)
    return (mixed_out[None], query_grad[None], key_grad[None], value_grad[None], weight_grad)


def solution(mesh):
    return jax.shard_map(
        local,
        mesh=mesh,
        in_specs=(
            P("dp", "seq", None),
            P("dp", "seq", None),
            P("dp", "seq", None),
            P("dp", "seq", None),
            P("dp", None),
            P("seq", "dp"),
        ),
        out_specs=(
            P("dp", "seq", None),
            P("dp", "seq", None),
            P("dp", "seq", None),
            P("dp", "seq", None),
            P("seq", "dp"),
        ),
        check_vma=False,
    )
```

```python
import jax
import jax.numpy as jnp
from jax import lax
from jax.sharding import PartitionSpec as P

HEADS = 12
HEAD_DIM = 64
STRETCH = 128
MOST = 1024


MASKED_SCORE = -1e30


def shift_up(block, axis, distance):
    devices = range(lax.axis_size(axis))
    route = [(i - distance, i) for i in devices if i - distance in devices]
    return lax.ppermute(block, axis, route)


def swap_partner(block, axis):
    count = lax.axis_size(axis)
    return lax.ppermute(block, axis, [(i, i ^ 1) for i in range(count)])


def frame_labels(utt_lengths, first_frame, frame_count, total_frames):
    positions = first_frame + jnp.arange(frame_count, dtype=jnp.int32)
    utt_ends = jnp.cumsum(utt_lengths)
    utt_index = jnp.sum((positions[:, None] >= utt_ends[None, :]).astype(jnp.int32), axis=1)
    outside = (positions < 0) | (positions >= total_frames)
    return (jnp.where(outside, -1, utt_index), positions // STRETCH)


def head_major(rows, tok_rows):
    return jnp.transpose(rows.reshape(tok_rows, HEADS, HEAD_DIM), (1, 0, 2))


def row_major(heads, tok_rows):
    return jnp.transpose(heads, (1, 0, 2)).reshape(tok_rows, HEADS * HEAD_DIM)


def gather_behind(own, reach, paired, core):
    if not paired:
        held = [own]
        for _ in range(reach):
            held.append(shift_up(held[-1], "seq", 1))
        return held
    evens = {0: own}
    count = lax.axis_size("seq")
    if reach == 4 and count % 4 == 0:
        row = (lax.axis_index("seq") // 2) % 2
        later = [i for i in range(count) if (i // 2) % 2 == 1]
        earlier = [i for i in range(count) if (i // 2) % 2 == 0 and i + 2 < count]
        far = [shift_up(own[k], "seq", 4) for k in range(2)]
        near = []
        for k in range(2):
            direct = lax.ppermute(own[k], "seq", [(i - 2, i) for i in later])
            relayed = lax.ppermute(far[k], "seq", [(i + 2, i) for i in earlier])
            near.append(jnp.where(row == 1, direct, relayed))
        evens[2] = jnp.stack(near)
        evens[4] = jnp.stack(far)
    else:
        for dist in range(2, reach + 2, 2):
            evens[dist] = shift_up(own, "seq", dist)
    odds = list(range(1, reach + 1, 2))
    payload = [jnp.where(core == 0, evens[s - 1], evens[s + 1]) for s in odds]
    received = swap_partner(payload, "seq")
    held = []
    for dist in range(reach + 1):
        held.append(evens[dist] if dist % 2 == 0 else received[(dist - 1) // 2])
    return held


def return_behind(parts, reach, paired, core):
    if not paired:
        carried = parts[reach]
        for dist in range(reach - 1, -1, -1):
            carried = shift_up(carried.astype(jnp.bfloat16), "seq", -1).astype(jnp.float32) + parts[dist]
        return carried
    odds = list(range(1, reach + 1, 2))
    received = swap_partner([parts[s] for s in odds], "seq")
    summed = {}
    for dist in range(0, reach + 2, 2):
        zero = jnp.zeros_like(parts[0])
        from_core1 = received[dist // 2] if dist // 2 < len(odds) else zero
        from_core0 = received[dist // 2 - 1] if dist >= 2 and dist // 2 - 1 < len(odds) else zero
        own = parts[dist] if dist <= reach else zero
        summed[dist] = own + jnp.where(core == 0, from_core1, from_core0)
    count = lax.axis_size("seq")
    if reach == 4 and count % 4 == 0:
        row = (lax.axis_index("seq") // 2) % 2
        later = [i for i in range(count) if (i // 2) % 2 == 1]
        earlier = [i for i in range(count) if (i // 2) % 2 == 0 and i + 2 < count]
        near = summed[2].astype(jnp.bfloat16)
        direct = lax.ppermute(near, "seq", [(i, i - 2) for i in later])
        relayed = lax.ppermute(near, "seq", [(i, i + 2) for i in earlier])
        far = summed[4] + jnp.where(row == 1, relayed.astype(jnp.float32), 0.0)
        total = summed[0] + jnp.where(row == 0, direct.astype(jnp.float32), 0.0)
        return total + shift_up(far.astype(jnp.bfloat16), "seq", -4).astype(jnp.float32)
    total = summed[0]
    for dist in range(2, reach + 2, 2):
        total = total + shift_up(summed[dist].astype(jnp.bfloat16), "seq", -dist).astype(jnp.float32)
    return total


def local(query_rows, key_rows, value_rows, out_grad, lengths, out_weight):
    seq_count = lax.axis_size("seq")
    device = lax.axis_index("seq")
    core = device % 2
    paired = seq_count % 2 == 0
    tok_rows = query_rows.shape[1]
    feature_width = query_rows.shape[2]
    total_frames = seq_count * tok_rows
    reach = min(-(-MOST // tok_rows), seq_count - 1)
    score_scale = HEAD_DIM ** (-0.5)
    utt_lengths = lengths[0]

    row_blocks, col_blocks = lax.axis_size("seq"), lax.axis_size("dp")
    pieces = lax.all_gather(out_weight, ("seq", "dp"), axis=0, tiled=False)
    weight_full = jnp.transpose(
        pieces.reshape((row_blocks, col_blocks) + out_weight.shape), (0, 2, 1, 3)
    ).reshape(row_blocks * out_weight.shape[0], col_blocks * out_weight.shape[1])

    query_heads = head_major(query_rows[0], tok_rows)
    own_kv = jnp.stack([head_major(key_rows[0], tok_rows), head_major(value_rows[0], tok_rows)])
    held = gather_behind(own_kv, reach, paired, core)

    query_utt, query_stretch = frame_labels(utt_lengths, device * tok_rows, tok_rows, total_frames)
    block_visible = []
    for dist in range(reach + 1):
        key_utt, key_stretch = frame_labels(
            utt_lengths, (device - dist) * tok_rows, tok_rows, total_frames
        )
        block_visible.append(
            (query_utt[:, None] == key_utt[None, :]) & (key_stretch[None, :] <= query_stretch[:, None])
        )

    block_scores = []
    top_score = None
    for dist in range(reach + 1):
        scores = (
            jnp.einsum("hqe,hke->hqk", query_heads, held[dist][0], preferred_element_type=jnp.float32)
            * score_scale
        )
        scores = jnp.where(block_visible[dist][None], scores, MASKED_SCORE)
        block_scores.append(scores)
        block_top = jnp.max(scores, axis=2)
        top_score = block_top if top_score is None else jnp.maximum(top_score, block_top)
    row_sum = None
    weighted = None
    for dist in range(reach + 1):
        expo_full = jnp.where(
            block_visible[dist][None], jnp.exp(block_scores[dist] - top_score[:, :, None]), 0.0
        )
        part_sum = jnp.sum(expo_full, axis=2)
        product = jnp.einsum(
            "hqk,hke->hqe",
            expo_full.astype(jnp.bfloat16),
            held[dist][1],
            preferred_element_type=jnp.float32,
        )
        row_sum = part_sum if row_sum is None else row_sum + part_sum
        weighted = product if weighted is None else weighted + product
    attended_heads = (weighted / row_sum[:, :, None]).astype(jnp.bfloat16)
    attended = row_major(attended_heads, tok_rows)
    log_sum = top_score + jnp.log(row_sum)

    upstream = out_grad[0]
    partial_weight = lax.dot_general(
        attended, upstream, (((0,), (0,)), ((), ())), preferred_element_type=jnp.float32
    )
    partial_weight, attended = lax.optimization_barrier((partial_weight, attended))
    att_grad = lax.dot_general(
        upstream, weight_full, (((1,), (1,)), ((), ())), preferred_element_type=jnp.float32
    ).astype(jnp.bfloat16)

    row_share = lax.psum_scatter(
        partial_weight.astype(jnp.bfloat16), "seq", scatter_dimension=0, tiled=True
    )
    weight_grad = lax.psum_scatter(
        row_share.astype(jnp.float32), "dp", scatter_dimension=1, tiled=True
    )

    grad_heads = head_major(att_grad, tok_rows)
    delta_rows = jnp.sum(
        grad_heads.astype(jnp.float32) * attended_heads.astype(jnp.float32), axis=2
    )

    query_acc = None
    parts = [None] * (reach + 1)
    order = [d for d in range(reach, -1, -1) if d % 2 == 1] + [
        d for d in range(2, reach + 1, 2)
    ] + [0]
    for dist in order:
        key_block = held[dist][0]
        value_block = held[dist][1]
        scores = (
            jnp.einsum("hqe,hke->hqk", query_heads, key_block, preferred_element_type=jnp.float32)
            * score_scale
        )
        prob_full = jnp.where(
            block_visible[dist][None], jnp.exp(scores - log_sum[:, :, None]), 0.0
        )
        prob_back = prob_full.astype(jnp.bfloat16)
        prob_grad = jnp.einsum(
            "hqe,hke->hqk", grad_heads, value_block, preferred_element_type=jnp.float32
        )
        score_grad = (prob_full * (prob_grad - delta_rows[:, :, None])).astype(jnp.bfloat16)
        query_part = jnp.einsum(
            "hqk,hke->hqe", score_grad, key_block, preferred_element_type=jnp.float32
        )
        query_acc = query_part if query_acc is None else query_acc + query_part
        key_part = (
            jnp.einsum("hqk,hqe->hke", score_grad, query_heads, preferred_element_type=jnp.float32)
            * score_scale
        )
        value_part = jnp.einsum(
            "hqk,hqe->hke", prob_back, grad_heads, preferred_element_type=jnp.float32
        )
        parts[dist] = jnp.stack([key_part, value_part])

    attended, parts = lax.optimization_barrier((attended, parts))
    kv_grad = return_behind(parts, reach, paired, core)
    mixed_out = jnp.dot(attended, weight_full, preferred_element_type=jnp.float32).astype(
        jnp.bfloat16
    )
    query_grad = row_major(query_acc * score_scale, tok_rows).astype(jnp.bfloat16)
    key_grad = row_major(kv_grad[0], tok_rows).astype(jnp.bfloat16)
    value_grad = row_major(kv_grad[1], tok_rows).astype(jnp.bfloat16)
    return (mixed_out[None], query_grad[None], key_grad[None], value_grad[None], weight_grad)


def solution(mesh):
    return jax.shard_map(
        local,
        mesh=mesh,
        in_specs=(
            P("dp", "seq", None),
            P("dp", "seq", None),
            P("dp", "seq", None),
            P("dp", "seq", None),
            P("dp", None),
            P("seq", "dp"),
        ),
        out_specs=(
            P("dp", "seq", None),
            P("dp", "seq", None),
            P("dp", "seq", None),
            P("dp", "seq", None),
            P("seq", "dp"),
        ),
        check_vma=False,
    )
```
